512 devices in a mesh: tm: 32 (over z, x_hi), fsdp: 16 (over y, x_lo, core).
Axes of the slice: x: 4 (x_hi: 2, x_lo: 2; x = x_hi * 2 + x_lo), y: 4, z: 16, core: 2. Of those that a mesh axis runs over, the one named last changes fastest.
Arguments:
- latents: bfloat16 [32768, 3072], P(('tm', 'fsdp')), may hold values from -6 to 6
- projected: bfloat16 [32768, 3, 2048], P(('tm', 'fsdp')), may hold values from -20 to 20
- out_weight: bfloat16 [2048, 3072], P(None, 'fsdp'), may hold values from -0.5 to 0.5
- gate_table: float32 [40, 3072], replicated, may hold values from 0.25 to 2
- timesteps: int32 [128], P('tm'), may hold values from 0 to 39
Outputs:
- updated: bfloat16 [32768, 3072], P(('tm', 'fsdp'))
The draws below stay inside these ranges and needn't reach their ends.
All inputs are finite; a program needn't handle non-finite values.
Results may differ from the reference program's by a relative error of at most 0.0085.
Values may be sent and summed in bfloat16 or wider, within the bound.
No kernel may reach another device: no remote copies, remote signals or barrier semaphores. Data moves between devices by JAX's collectives and lax.ppermute only.
A program may use at most 64 MiB of HBM per device.

```python
import math
import jax
import jax.numpy as jnp
from jax import lax

D = 3072
HEAD_DIM = 128
STEPS = 40
FRAME_TOK = 256
HEADS = 16
INNER = 2048
FRAMES = 128
TOKENS = 32768


def draw_projected(key, part):
    inner_width = HEADS * HEAD_DIM
    lanes = jnp.array([2.0, 1.0, 1.0], jnp.float32).reshape(1, 3, 1)
    sample = jnp.clip(jax.random.normal(key, (TOKENS, 3, inner_width), jnp.float32), -6.0, 6.0)
    sample = sample * lanes
    signs = jnp.where(jax.random.bernoulli(jax.random.fold_in(key, 11), 0.5, (TOKENS, inner_width)), 1.0, -1.0)
    earlier_signs = jnp.roll(signs, 1, axis=0)
    position = jnp.arange(TOKENS, dtype=jnp.int32)
    within = position % FRAME_TOK
    strength = jnp.array([9.0, 14.0, 20.0], jnp.float32)[position // FRAME_TOK % 3][:, None]
    anchor = (within == 5)[:, None]
    partner = (within == 6)[:, None]
    lifted = 1.0 + 2.0 / (strength * math.sqrt(HEAD_DIM))
    query_part = jnp.where(anchor, strength * signs, sample[:, 0])
    key_part = jnp.where(anchor, signs, jnp.where(partner, earlier_signs * lifted, sample[:, 1]))
    return jnp.stack([query_part, key_part, sample[:, 2]], axis=1).astype(jnp.bfloat16)


def touch_ends(values, rng, low, top_value):
    dims = values.shape
    index_at = [jax.random.randint(jax.random.fold_in(rng, axis), (), 0, dims[axis]) for axis in range(len(dims))]
    values = values.at[tuple(index_at)].set(low)
    longest = dims.index(max(dims))
    index_at[longest] = (index_at[longest] + 1) % dims[longest]
    return values.at[tuple(index_at)].set(top_value)


def steps_of(key, extent, pieces, low, top_value):
    def one(dim, parts):
        draws = jax.random.uniform(jax.random.fold_in(jax.random.fold_in(key, 6), dim), (parts,), jnp.float32, low / len(pieces), top_value / len(pieces))
        return jnp.repeat(jnp.exp(draws), extent[dim] // parts).reshape((-1,) + (1,) * (len(extent) - dim - 1))

    factor_of = one(*pieces[0])
    for cut in pieces[1:]:
        factor_of = factor_of * one(*cut)
    return factor_of


def normal_values(rng, extent, scale, reach, cuts=(), kind=jnp.bfloat16):
    gain = steps_of(rng, extent, cuts, -0.22, 0.18) if cuts else 1.0
    entries = jax.random.normal(rng, extent, jnp.float32) * scale * gain
    return jnp.minimum(jnp.maximum(entries, -reach), reach).astype(kind)


def setup_inputs(seed: int = 0) -> dict:
    streams_of = jax.random.split(jax.random.key(seed), 6)
    return {
        "latents": normal_values(streams_of[0], (TOKENS, D), 1.0, 6.0, ((0, 512),)),
        "projected": draw_projected(jax.random.fold_in(streams_of[5], 71), 0),
        "out_weight": normal_values(streams_of[2], (INNER, D), HEAD_DIM ** -0.5, 0.5, ((1, 16),)),
        "gate_table": jnp.clip(jax.random.uniform(streams_of[3], (STEPS, D), jnp.float32, 0.25, 2.0), 0.25, 2.0),
        "timesteps": touch_ends(jax.random.randint(streams_of[4], (FRAMES,), 0, STEPS), jax.random.fold_in(streams_of[4], 1), 0, STEPS - 1).astype(jnp.int32),
    }


def reference(latents, projected, out_weight, gate_table, timesteps):
    frame_count = timesteps.shape[0]
    head_count = projected.shape[2] // HEAD_DIM
    grouped = projected.reshape(frame_count, FRAME_TOK, 3, head_count, HEAD_DIM)
    padded = jnp.concatenate([jnp.zeros((3, FRAME_TOK, 3, head_count, HEAD_DIM), projected.dtype), grouped], axis=0)
    score_scale = HEAD_DIM ** -0.5
    key_frame = jnp.arange(4 * FRAME_TOK, dtype=jnp.int32) // FRAME_TOK
    residual = latents.reshape(frame_count, FRAME_TOK, latents.shape[1])

    def one_frame(frame_index):
        window = lax.dynamic_slice_in_dim(padded, frame_index, 4, 0)
        queries = window[3, :, 0].astype(jnp.float32)
        key_rows = window[:, :, 1].reshape(4 * FRAME_TOK, head_count, HEAD_DIM).astype(jnp.float32)
        value_rows = window[:, :, 2].reshape(4 * FRAME_TOK, head_count, HEAD_DIM).astype(jnp.float32)
        scores = jnp.einsum("qhd,khd->hqk", queries, key_rows) * score_scale
        valid = (frame_index - 3 + key_frame) >= 0
        scores = jnp.where(valid[None, None, :], scores, -1e30)
        row_max = jnp.max(scores, axis=-1, keepdims=True)
        weights = jnp.exp(scores - row_max)
        row_sum = jnp.sum(weights, axis=-1, keepdims=True)
        probability = (weights / row_sum).astype(jnp.bfloat16)
        attended = jnp.einsum("hqk,khd->qhd", probability.astype(jnp.float32), value_rows).astype(jnp.bfloat16)
        attended = attended.reshape(FRAME_TOK, head_count * HEAD_DIM)
        branch = jnp.dot(attended, out_weight, preferred_element_type=jnp.float32)
        gate_row = lax.dynamic_index_in_dim(gate_table, timesteps[frame_index], 0, keepdims=True)
        frame_latents = lax.dynamic_index_in_dim(residual, frame_index, 0, keepdims=False)
        return (frame_latents.astype(jnp.float32) + gate_row * branch).astype(jnp.bfloat16)

    stacked = lax.map(one_frame, jnp.arange(frame_count, dtype=jnp.int32))
    return stacked.reshape(frame_count * FRAME_TOK, latents.shape[1])
```

```python
import jax
import jax.numpy as jnp
from jax import lax
from jax.experimental import pallas as pl
from jax.experimental.pallas import tpu as pltpu
from jax.sharding import Mesh
from jax.sharding import PartitionSpec as P

FRAME_TOK = 256
WINDOW = 4


def passed_along(value, axis, steps):
    count = lax.axis_size(axis)
    initial, last = (max(0, -steps), min(count, count - steps))
    return lax.ppermute(value, axis, [(source, source + steps) for source in range(initial, last)])


def attention_kernel(flag_ref, qkv_ref, halo_ref, out_ref):
    frame_count = qkv_ref.shape[1] // FRAME_TOK
    score_scale = qkv_ref.shape[2] ** (-0.5)
    has_prev = flag_ref[0] > 0
    for frame in range(frame_count):
        query = qkv_ref[0, pl.ds(frame * FRAME_TOK, FRAME_TOK), :]
        blocks = []
        for back in range(WINDOW):
            source = frame - (WINDOW - 1) + back
            if source >= 0:
                rows = pl.ds(source * FRAME_TOK, FRAME_TOK)
                key, value = qkv_ref[1, rows, :], qkv_ref[2, rows, :]
            else:
                rows = pl.ds((source + WINDOW - 1) * FRAME_TOK, FRAME_TOK)
                key, value = halo_ref[0, rows, :], halo_ref[1, rows, :]
            scores = (
                lax.dot_general(
                    query, key, (((1,), (1,)), ((), ())), preferred_element_type=jnp.float32
                )
                * score_scale
            )
            if source < 0:
                scores = jnp.where(has_prev, scores, -1e30)
            blocks.append((scores, value))
        row_max = blocks[0][0].max(axis=1, keepdims=True)
        for scores, _ in blocks[1:]:
            row_max = jnp.maximum(row_max, scores.max(axis=1, keepdims=True))
        weights = [jnp.exp(scores - row_max) for scores, _ in blocks]
        row_sum = weights[0].sum(axis=1, keepdims=True)
        for w in weights[1:]:
            row_sum = row_sum + w.sum(axis=1, keepdims=True)
        inverse = 1.0 / row_sum
        total = None
        for w, (_, value) in zip(weights, blocks):
            probability = (w * inverse).astype(jnp.bfloat16)
            part = jnp.dot(probability, value, preferred_element_type=jnp.float32)
            total = part if total is None else total + part
        out_ref[pl.ds(frame * FRAME_TOK, FRAME_TOK), :] = total.astype(out_ref.dtype)


def attend(flag, qkv, halo):
    tokens, width = qkv.shape[1], qkv.shape[2]
    vmem = pl.BlockSpec(memory_space=pltpu.VMEM)
    return pl.pallas_call(
        attention_kernel,
        out_shape=jax.ShapeDtypeStruct((tokens, width), jnp.bfloat16),
        in_specs=[pl.BlockSpec(memory_space=pltpu.SMEM), vmem, vmem],
        out_specs=vmem,
    )(flag, qkv, halo)


def body(latents, projected, out_weight, gate_table, timesteps):
    row_count = latents.shape[0]
    frame_count = timesteps.shape[0]
    outer = lax.axis_size("fo")
    inner = lax.axis_size("fc")
    head_dim = projected.shape[2] // (outer * inner)
    shard = lax.axis_index("fo") * inner + lax.axis_index("fc")

    head_view = lax.all_to_all(projected, ("fo", "fc"), split_axis=2, concat_axis=0, tiled=True)
    qkv = jnp.transpose(head_view, (1, 0, 2))
    halo = passed_along(qkv[1:3, FRAME_TOK:], "tm", 1)
    flag = (lax.axis_index("tm") > 0).astype(jnp.int32).reshape(1)
    attended = attend(flag, qkv, halo)

    split = attended.reshape(outer, inner, row_count, head_dim)
    split = lax.all_to_all(split, "fc", split_axis=1, concat_axis=1, tiled=True)
    gathered = lax.all_gather(split, "fo", axis=0, tiled=False)
    columns = lax.all_gather(out_weight, "fc", axis=1, tiled=True)
    columns = columns.reshape(outer, inner, head_dim, columns.shape[1])
    partial = jnp.einsum(
        "aibrd,abdn->irn", gathered, columns, preferred_element_type=jnp.float32
    ).astype(jnp.bfloat16)
    returned = lax.all_to_all(partial, "fo", split_axis=0, concat_axis=0, tiled=True)
    branch = jnp.transpose(returned, (1, 0, 2)).reshape(row_count, -1)

    frame_index = (shard * row_count) // FRAME_TOK
    gate_row = gate_table[timesteps[frame_index]]
    updated = latents.astype(jnp.float32) + gate_row[None, :] * branch.astype(jnp.float32)
    return updated.astype(jnp.bfloat16)


def solution(mesh):
    tm_size, fsdp_size = mesh.devices.shape
    split_mesh = Mesh(mesh.devices.reshape(tm_size, fsdp_size // 2, 2), ("tm", "fo", "fc"))
    rows = ("tm", "fo", "fc")
    in_specs = (
        P(rows, None),
        P(rows, None, None),
        P(None, ("fo", "fc")),
        P(),
        P("tm"),
    )
    out_specs = P(rows, None)
    return jax.shard_map(
        body, mesh=split_mesh, in_specs=in_specs, out_specs=out_specs, check_vma=False
    )
```

```python
import jax
import jax.numpy as jnp
from jax import lax
from jax.experimental import pallas as pl
from jax.experimental.pallas import tpu as pltpu
from jax.sharding import Mesh
from jax.sharding import PartitionSpec as P

FRAME_TOK = 256
WINDOW = 4


def passed_along(value, axis, steps):
    count = lax.axis_size(axis)
    initial, last = (max(0, -steps), min(count, count - steps))
    return lax.ppermute(value, axis, [(source, source + steps) for source in range(initial, last)])


def attention_kernel(flag_ref, qkv_ref, halo_ref, out_ref):
    frame_count = qkv_ref.shape[1] // FRAME_TOK
    score_scale = qkv_ref.shape[2] ** (-0.5)
    has_prev = flag_ref[0] > 0
    for frame in range(frame_count):
        query = qkv_ref[0, pl.ds(frame * FRAME_TOK, FRAME_TOK), :]
        blocks = []
        for back in range(WINDOW):
            source = frame - (WINDOW - 1) + back
            if source >= 0:
                rows = pl.ds(source * FRAME_TOK, FRAME_TOK)
                key, value = qkv_ref[1, rows, :], qkv_ref[2, rows, :]
            else:
                rows = pl.ds((source + WINDOW - 1) * FRAME_TOK, FRAME_TOK)
                key, value = halo_ref[0, rows, :], halo_ref[1, rows, :]
            scores = (
                lax.dot_general(
                    query, key, (((1,), (1,)), ((), ())), preferred_element_type=jnp.float32
                )
                * score_scale
            )
            if source < 0:
                scores = jnp.where(has_prev, scores, -1e30)
            blocks.append((scores, value))
        row_max = blocks[0][0].max(axis=1, keepdims=True)
        for scores, _ in blocks[1:]:
            row_max = jnp.maximum(row_max, scores.max(axis=1, keepdims=True))
        weights = [jnp.exp(scores - row_max) for scores, _ in blocks]
        row_sum = weights[0].sum(axis=1, keepdims=True)
        for w in weights[1:]:
            row_sum = row_sum + w.sum(axis=1, keepdims=True)
        inverse = 1.0 / row_sum
        total = None
        for w, (_, value) in zip(weights, blocks):
            probability = (w * inverse).astype(jnp.bfloat16)
            part = jnp.dot(probability, value, preferred_element_type=jnp.float32)
            total = part if total is None else total + part
        out_ref[pl.ds(frame * FRAME_TOK, FRAME_TOK), :] = total.astype(out_ref.dtype)


def attend(flag, qkv, halo):
    tokens, width = qkv.shape[1], qkv.shape[2]
    vmem = pl.BlockSpec(memory_space=pltpu.VMEM)
    return pl.pallas_call(
        attention_kernel,
        out_shape=jax.ShapeDtypeStruct((tokens, width), jnp.bfloat16),
        in_specs=[pl.BlockSpec(memory_space=pltpu.SMEM), vmem, vmem],
        out_specs=vmem,
    )(flag, qkv, halo)


def shifted_copies(value, axis):
    count = lax.axis_size(axis)
    copies = [value]
    for shift in range(1, count):
        pairs = [(source, (source + shift) % count) for source in range(count)]
        copies.append(lax.ppermute(value, axis, pairs))
    return copies


def body(latents, projected, out_weight, gate_table, timesteps):
    row_count = latents.shape[0]
    outer = lax.axis_size("fy")
    inner = lax.axis_size("fp")
    head_dim = projected.shape[2] // (outer * inner)
    me_outer = lax.axis_index("fy")
    shard = me_outer * inner + lax.axis_index("fp")

    columns = lax.all_gather(out_weight, "fp", axis=1, tiled=True)
    columns = columns.reshape(outer, inner, head_dim, columns.shape[1])

    head_view = lax.all_to_all(projected, ("fy", "fp"), split_axis=2, concat_axis=0, tiled=True)
    qkv = jnp.transpose(head_view, (1, 0, 2))
    halo = passed_along(qkv[1:3, FRAME_TOK:], "tm", 1)
    flag = (lax.axis_index("tm") > 0).astype(jnp.int32).reshape(1)
    attended = attend(flag, qkv, halo)

    split = attended.reshape(outer, inner, row_count, head_dim)
    split = lax.all_to_all(split, "fp", split_axis=1, concat_axis=1, tiled=True)
    total = None
    for shift, part in enumerate(shifted_copies(split, "fy")):
        source = (me_outer - shift) % outer
        weight = lax.dynamic_index_in_dim(columns, source, 0, keepdims=False)
        piece = jnp.einsum("ibrd,bdn->irn", part, weight, preferred_element_type=jnp.float32)
        total = piece if total is None else total + piece
    returned = lax.all_to_all(total.astype(jnp.bfloat16), "fy", split_axis=0, concat_axis=0, tiled=True)
    branch = jnp.transpose(returned, (1, 0, 2)).reshape(row_count, -1)

    frame_index = (shard * row_count) // FRAME_TOK
    gate_row = gate_table[timesteps[frame_index]]
    updated = latents.astype(jnp.float32) + gate_row[None, :] * branch.astype(jnp.float32)
    return updated.astype(jnp.bfloat16)


def solution(mesh):
    tm_size, fsdp_size = mesh.devices.shape
    split_mesh = Mesh(mesh.devices.reshape(tm_size, fsdp_size // 4, 4), ("tm", "fy", "fp"))
    rows = ("tm", "fy", "fp")
    in_specs = (
        P(rows, None),
        P(rows, None, None),
        P(None, ("fy", "fp")),
        P(),
        P("tm"),
    )
    out_specs = P(rows, None)
    return jax.shard_map(
        body, mesh=split_mesh, in_specs=in_specs, out_specs=out_specs, check_vma=False
    )
```

```python
import jax
import jax.numpy as jnp
from jax import lax
from jax.experimental import pallas as pl
from jax.experimental.pallas import tpu as pltpu
from jax.sharding import Mesh
from jax.sharding import PartitionSpec as P

FRAME_TOK = 256
WINDOW = 4


def passed_along(value, axis, steps):
    count = lax.axis_size(axis)
    initial, last = (max(0, -steps), min(count, count - steps))
    return lax.ppermute(value, axis, [(source, source + steps) for source in range(initial, last)])


def attention_kernel(flag_ref, qkv_ref, halo_ref, out_ref):
    row_count = qkv_ref.shape[2]
    per_frame = FRAME_TOK // row_count
    frame_count = qkv_ref.shape[0] // per_frame
    score_scale = qkv_ref.shape[3] ** (-0.5)
    outer, inner = out_ref.shape[0] // out_ref.shape[1], out_ref.shape[1]
    has_prev = flag_ref[0] > 0

    def frame_rows(ref, block, plane):
        return ref[pl.ds(block, per_frame), plane].reshape(FRAME_TOK, ref.shape[3])

    for frame in range(frame_count):
        query = frame_rows(qkv_ref, frame * per_frame, 0)
        blocks = []
        for back in range(WINDOW):
            source = frame - (WINDOW - 1) + back
            if source >= 0:
                key = frame_rows(qkv_ref, source * per_frame, 1)
                value = frame_rows(qkv_ref, source * per_frame, 2)
            else:
                block = (source + WINDOW - 1) * per_frame
                key, value = frame_rows(halo_ref, block, 0), frame_rows(halo_ref, block, 1)
            scores = (
                lax.dot_general(
                    query, key, (((1,), (1,)), ((), ())), preferred_element_type=jnp.float32
                )
                * score_scale
            )
            if source < 0:
                scores = jnp.where(has_prev, scores, -1e30)
            blocks.append((scores, value))
        row_max = blocks[0][0].max(axis=1, keepdims=True)
        for scores, _ in blocks[1:]:
            row_max = jnp.maximum(row_max, scores.max(axis=1, keepdims=True))
        weights = [jnp.exp(scores - row_max) for scores, _ in blocks]
        row_sum = weights[0].sum(axis=1, keepdims=True)
        for w in weights[1:]:
            row_sum = row_sum + w.sum(axis=1, keepdims=True)
        inverse = 1.0 / row_sum
        total = None
        for w, (_, value) in zip(weights, blocks):
            probability = (w * inverse).astype(jnp.bfloat16)
            part = jnp.dot(probability, value, preferred_element_type=jnp.float32)
            total = part if total is None else total + part
        total = total.astype(out_ref.dtype)
        for piece in range(per_frame):
            row_outer, row_inner = divmod(frame * per_frame + piece, inner)
            rows = total[piece * row_count : (piece + 1) * row_count]
            for dest_outer in range(outer):
                out_ref[dest_outer * inner + row_inner, row_outer] = rows


def attend(flag, qkv, halo, outer, inner):
    row_count, width = qkv.shape[2], qkv.shape[3]
    vmem = pl.BlockSpec(memory_space=pltpu.VMEM)
    return pl.pallas_call(
        attention_kernel,
        out_shape=jax.ShapeDtypeStruct((outer * inner, outer, row_count, width), jnp.bfloat16),
        in_specs=[pl.BlockSpec(memory_space=pltpu.SMEM), vmem, vmem],
        out_specs=vmem,
    )(flag, qkv, halo)


def chunk_kernel(rows_ref, out_ref):
    width = out_ref.shape[3]
    for head in range(out_ref.shape[0]):
        out_ref[head] = rows_ref[:, :, head * width : (head + 1) * width]


def head_chunks(planes, heads):
    lanes, row_count, features = planes.shape
    vmem = pl.BlockSpec(memory_space=pltpu.VMEM)
    return pl.pallas_call(
        chunk_kernel,
        out_shape=jax.ShapeDtypeStruct((heads, lanes, row_count, features // heads), planes.dtype),
        in_specs=[vmem],
        out_specs=vmem,
    )(planes)


def body(latents, projected, out_weight, gate_table, timesteps):
    row_count = latents.shape[0]
    outer = lax.axis_size("fy")
    inner = lax.axis_size("fp")
    heads = outer * inner
    head_dim = projected.shape[2] // heads
    per_frame = FRAME_TOK // row_count
    shard = lax.axis_index("fy") * inner + lax.axis_index("fp")

    columns = lax.all_gather(out_weight, "fp", axis=1, tiled=True)
    columns = columns.reshape(heads, head_dim, columns.shape[1])

    chunks = head_chunks(jnp.transpose(projected, (1, 0, 2)), heads)
    qkv = lax.all_to_all(chunks, ("fy", "fp"), split_axis=0, concat_axis=0, tiled=True)
    halo = passed_along(qkv[per_frame:, 1:3], "tm", 1)
    flag = (lax.axis_index("tm") > 0).astype(jnp.int32).reshape(1)
    spread = attend(flag, qkv, halo, outer, inner)

    gathered = lax.all_to_all(spread, ("fy", "fp"), split_axis=0, concat_axis=0, tiled=True)
    total = jnp.einsum("jird,jdn->irn", gathered, columns, preferred_element_type=jnp.float32)
    returned = lax.all_to_all(total.astype(jnp.bfloat16), "fy", split_axis=0, concat_axis=0, tiled=True)
    branch = jnp.transpose(returned, (1, 0, 2)).reshape(row_count, -1)

    frame_index = (shard * row_count) // FRAME_TOK
    gate_row = gate_table[timesteps[frame_index]]
    updated = latents.astype(jnp.float32) + gate_row[None, :] * branch.astype(jnp.float32)
    return updated.astype(jnp.bfloat16)


def solution(mesh):
    tm_size, fsdp_size = mesh.devices.shape
    split_mesh = Mesh(mesh.devices.reshape(tm_size, fsdp_size // 4, 4), ("tm", "fy", "fp"))
    rows = ("tm", "fy", "fp")
    in_specs = (
        P(rows, None),
        P(rows, None, None),
        P(None, ("fy", "fp")),
        P(),
        P("tm"),
    )
    out_specs = P(rows, None)
    return jax.shard_map(
        body, mesh=split_mesh, in_specs=in_specs, out_specs=out_specs, check_vma=False
    )
```

```python
import jax
import jax.numpy as jnp
from jax import lax
from jax.experimental import pallas as pl
from jax.experimental.pallas import tpu as pltpu
from jax.sharding import Mesh
from jax.sharding import PartitionSpec as P

FRAME_TOK = 256
WINDOW = 4


def passed_along(value, axis, steps):
    count = lax.axis_size(axis)
    initial, last = (max(0, -steps), min(count, count - steps))
    return lax.ppermute(value, axis, [(source, source + steps) for source in range(initial, last)])


def attention_kernel(flag_ref, qkv_ref, halo_ref, out_ref):
    row_count = qkv_ref.shape[2]
    per_frame = FRAME_TOK // row_count
    frame_count = qkv_ref.shape[0] // per_frame
    score_scale = qkv_ref.shape[3] ** (-0.5)
    inner = out_ref.shape[0] // frame_count
    has_prev = flag_ref[0] > 0

    def frame_rows(ref, block, plane):
        return ref[pl.ds(block, per_frame), plane].reshape(FRAME_TOK, ref.shape[3])

    for frame in range(frame_count):
        query = frame_rows(qkv_ref, frame * per_frame, 0)
        blocks = []
        for back in range(WINDOW):
            source = frame - (WINDOW - 1) + back
            if source >= 0:
                key = frame_rows(qkv_ref, source * per_frame, 1)
                value = frame_rows(qkv_ref, source * per_frame, 2)
            else:
                block = (source + WINDOW - 1) * per_frame
                key, value = frame_rows(halo_ref, block, 0), frame_rows(halo_ref, block, 1)
            scores = (
                lax.dot_general(
                    query, key, (((1,), (1,)), ((), ())), preferred_element_type=jnp.float32
                )
                * score_scale
            )
            if source < 0:
                scores = jnp.where(has_prev, scores, -1e30)
            blocks.append((scores, value))
        row_max = blocks[0][0].max(axis=1, keepdims=True)
        for scores, _ in blocks[1:]:
            row_max = jnp.maximum(row_max, scores.max(axis=1, keepdims=True))
        weights = [jnp.exp(scores - row_max) for scores, _ in blocks]
        row_sum = weights[0].sum(axis=1, keepdims=True)
        for w in weights[1:]:
            row_sum = row_sum + w.sum(axis=1, keepdims=True)
        inverse = 1.0 / row_sum
        total = None
        for w, (_, value) in zip(weights, blocks):
            probability = (w * inverse).astype(jnp.bfloat16)
            part = jnp.dot(probability, value, preferred_element_type=jnp.float32)
            total = part if total is None else total + part
        total = total.astype(out_ref.dtype)
        for dest in range(frame * inner, (frame + 1) * inner):
            out_ref[dest] = total


def attend(flag, qkv, halo, outer, inner):
    width = qkv.shape[3]
    vmem = pl.BlockSpec(memory_space=pltpu.VMEM)
    return pl.pallas_call(
        attention_kernel,
        out_shape=jax.ShapeDtypeStruct((outer * inner, FRAME_TOK, width), jnp.bfloat16),
        in_specs=[pl.BlockSpec(memory_space=pltpu.SMEM), vmem, vmem],
        out_specs=vmem,
    )(flag, qkv, halo)


def chunk_kernel(rows_ref, out_ref):
    width = out_ref.shape[3]
    for head in range(out_ref.shape[0]):
        out_ref[head] = rows_ref[:, :, head * width : (head + 1) * width]


def head_chunks(planes, heads):
    lanes, row_count, features = planes.shape
    vmem = pl.BlockSpec(memory_space=pltpu.VMEM)
    return pl.pallas_call(
        chunk_kernel,
        out_shape=jax.ShapeDtypeStruct((heads, lanes, row_count, features // heads), planes.dtype),
        in_specs=[vmem],
        out_specs=vmem,
    )(planes)


def projection_kernel(gathered_ref, weight_ref, out_ref):
    heads, head_dim = gathered_ref.shape[0], gathered_ref.shape[2]
    total = None
    for head in range(heads):
        part = lax.dot_general(
            gathered_ref[head],
            weight_ref[:, head * head_dim : (head + 1) * head_dim],
            (((1,), (1,)), ((), ())),
            preferred_element_type=jnp.float32,
        )
        total = part if total is None else total + part
    out_ref[...] = total.astype(out_ref.dtype)


def project(gathered, weight_t):
    vmem = pl.BlockSpec(memory_space=pltpu.VMEM)
    return pl.pallas_call(
        projection_kernel,
        out_shape=jax.ShapeDtypeStruct((gathered.shape[1], weight_t.shape[0]), jnp.bfloat16),
        in_specs=[vmem, vmem],
        out_specs=vmem,
    )(gathered, weight_t)


def body(latents, projected, out_weight, gate_table, timesteps):
    row_count = latents.shape[0]
    outer = lax.axis_size("fy")
    inner = lax.axis_size("fp")
    heads = outer * inner
    per_frame = FRAME_TOK // row_count
    shard = lax.axis_index("fy") * inner + lax.axis_index("fp")

    columns = lax.all_gather(out_weight, "fy", axis=1, tiled=True)

    chunks = head_chunks(jnp.transpose(projected, (1, 0, 2)), heads)
    qkv = lax.all_to_all(chunks, ("fy", "fp"), split_axis=0, concat_axis=0, tiled=True)
    halo = passed_along(qkv[per_frame:, 1:3], "tm", 1)
    flag = (lax.axis_index("tm") > 0).astype(jnp.int32).reshape(1)
    spread = attend(flag, qkv, halo, outer, inner)

    gathered = lax.all_to_all(spread, ("fy", "fp"), split_axis=0, concat_axis=0, tiled=True)
    total = project(gathered, jnp.transpose(columns))
    total = total.reshape(inner, row_count, total.shape[1])
    returned = lax.all_to_all(total, "fp", split_axis=0, concat_axis=0, tiled=True)
    width = out_weight.shape[1]
    branch = returned.reshape(inner, row_count, outer, width)
    branch = jnp.transpose(branch, (1, 2, 0, 3)).reshape(row_count, -1)

    frame_index = (shard * row_count) // FRAME_TOK
    gate_row = gate_table[timesteps[frame_index]]
    updated = latents.astype(jnp.float32) + gate_row[None, :] * branch.astype(jnp.float32)
    return updated.astype(jnp.bfloat16)


def solution(mesh):
    tm_size, fsdp_size = mesh.devices.shape
    split_mesh = Mesh(mesh.devices.reshape(tm_size, fsdp_size // 4, 4), ("tm", "fy", "fp"))
    rows = ("tm", "fy", "fp")
    in_specs = (
        P(rows, None),
        P(rows, None, None),
        P(None, ("fy", "fp")),
        P(),
        P("tm"),
    )
    out_specs = P(rows, None)
    return jax.shard_map(
        body, mesh=split_mesh, in_specs=in_specs, out_specs=out_specs, check_vma=False
    )
```

```python
import jax
import jax.numpy as jnp
from jax import lax
from jax.experimental import pallas as pl
from jax.experimental.pallas import tpu as pltpu
from jax.sharding import Mesh
from jax.sharding import PartitionSpec as P

FRAME_TOK = 256
WINDOW = 4


def passed_along(value, axis, steps):
    count = lax.axis_size(axis)
    initial, last = (max(0, -steps), min(count, count - steps))
    return lax.ppermute(value, axis, [(source, source + steps) for source in range(initial, last)])


def attention_kernel(flag_ref, qkv_ref, halo_ref, out_ref):
    row_count = qkv_ref.shape[2]
    per_frame = FRAME_TOK // row_count
    frame_count = qkv_ref.shape[0] // per_frame
    score_scale = qkv_ref.shape[3] ** (-0.5)
    outer = out_ref.shape[1]
    inner = out_ref.shape[0] // outer
    has_prev = flag_ref[0] > 0

    def frame_rows(ref, block, plane):
        return ref[pl.ds(block, per_frame), plane].reshape(FRAME_TOK, ref.shape[3])

    for frame in range(frame_count):
        query = frame_rows(qkv_ref, frame * per_frame, 0)
        blocks = []
        for back in range(WINDOW):
            source = frame - (WINDOW - 1) + back
            if source >= 0:
                key = frame_rows(qkv_ref, source * per_frame, 1)
                value = frame_rows(qkv_ref, source * per_frame, 2)
            else:
                block = (source + WINDOW - 1) * per_frame
                key, value = frame_rows(halo_ref, block, 0), frame_rows(halo_ref, block, 1)
            scores = (
                lax.dot_general(
                    query, key, (((1,), (1,)), ((), ())), preferred_element_type=jnp.float32
                )
                * score_scale
            )
            if source < 0:
                scores = jnp.where(has_prev, scores, -1e30)
            blocks.append((scores, value))
        row_max = blocks[0][0].max(axis=1, keepdims=True)
        for scores, _ in blocks[1:]:
            row_max = jnp.maximum(row_max, scores.max(axis=1, keepdims=True))
        weights = [jnp.exp(scores - row_max) for scores, _ in blocks]
        row_sum = weights[0].sum(axis=1, keepdims=True)
        for w in weights[1:]:
            row_sum = row_sum + w.sum(axis=1, keepdims=True)
        inverse = 1.0 / row_sum
        total = None
        for w, (_, value) in zip(weights, blocks):
            probability = (w * inverse).astype(jnp.bfloat16)
            part = jnp.dot(probability, value, preferred_element_type=jnp.float32)
            total = part if total is None else total + part
        total = total.astype(out_ref.dtype)
        for piece in range(per_frame):
            row_outer, row_inner = divmod(frame * per_frame + piece, inner)
            rows = total[piece * row_count : (piece + 1) * row_count]
            for dest_outer in range(outer):
                out_ref[dest_outer * inner + row_inner, row_outer] = rows


def attend(flag, qkv, halo, outer, inner):
    row_count, width = qkv.shape[2], qkv.shape[3]
    vmem = pl.BlockSpec(memory_space=pltpu.VMEM)
    return pl.pallas_call(
        attention_kernel,
        out_shape=jax.ShapeDtypeStruct((outer * inner, outer, row_count, width), jnp.bfloat16),
        in_specs=[pl.BlockSpec(memory_space=pltpu.SMEM), vmem, vmem],
        out_specs=vmem,
    )(flag, qkv, halo)


def chunk_kernel(rows_ref, out_ref):
    width = out_ref.shape[3]
    for head in range(out_ref.shape[0]):
        out_ref[head] = rows_ref[:, :, head * width : (head + 1) * width]


def head_chunks(planes, heads):
    lanes, row_count, features = planes.shape
    vmem = pl.BlockSpec(memory_space=pltpu.VMEM)
    return pl.pallas_call(
        chunk_kernel,
        out_shape=jax.ShapeDtypeStruct((heads, lanes, row_count, features // heads), planes.dtype),
        in_specs=[vmem],
        out_specs=vmem,
    )(planes)


def projection_kernel(gathered_ref, weight_ref, out_ref):
    heads, head_dim = gathered_ref.shape[0], gathered_ref.shape[3]
    total = None
    for head in range(heads):
        part = lax.dot_general(
            gathered_ref[head].reshape(-1, head_dim),
            weight_ref[:, head * head_dim : (head + 1) * head_dim],
            (((1,), (1,)), ((), ())),
            preferred_element_type=jnp.float32,
        )
        total = part if total is None else total + part
    out_ref[...] = total.astype(out_ref.dtype)


def project(gathered, weight_t):
    vmem = pl.BlockSpec(memory_space=pltpu.VMEM)
    return pl.pallas_call(
        projection_kernel,
        out_shape=jax.ShapeDtypeStruct(
            (gathered.shape[1] * gathered.shape[2], weight_t.shape[0]), jnp.bfloat16
        ),
        in_specs=[vmem, vmem],
        out_specs=vmem,
    )(gathered, weight_t)


def body(latents, projected, out_weight, gate_table, timesteps):
    row_count = latents.shape[0]
    outer = lax.axis_size("fo")
    inner = lax.axis_size("fc")
    heads = outer * inner
    per_frame = FRAME_TOK // row_count
    shard = lax.axis_index("fo") * inner + lax.axis_index("fc")

    columns = lax.all_gather(out_weight, "fc", axis=1, tiled=True)

    chunks = head_chunks(jnp.transpose(projected, (1, 0, 2)), heads)
    qkv = lax.all_to_all(chunks, ("fo", "fc"), split_axis=0, concat_axis=0, tiled=True)
    halo = passed_along(qkv[per_frame:, 1:3], "tm", 1)
    flag = (lax.axis_index("tm") > 0).astype(jnp.int32).reshape(1)
    spread = attend(flag, qkv, halo, outer, inner)

    gathered = lax.all_to_all(spread, ("fo", "fc"), split_axis=0, concat_axis=0, tiled=True)
    total = project(gathered, jnp.transpose(columns))
    total = total.reshape(outer, row_count, total.shape[1])
    returned = lax.all_to_all(total, "fo", split_axis=0, concat_axis=0, tiled=True)
    branch = jnp.transpose(returned, (1, 0, 2)).reshape(row_count, -1)

    frame_index = (shard * row_count) // FRAME_TOK
    gate_row = gate_table[timesteps[frame_index]]
    updated = latents.astype(jnp.float32) + gate_row[None, :] * branch.astype(jnp.float32)
    return updated.astype(jnp.bfloat16)


def solution(mesh):
    tm_size, fsdp_size = mesh.devices.shape
    split_mesh = Mesh(mesh.devices.reshape(tm_size, fsdp_size // 2, 2), ("tm", "fo", "fc"))
    rows = ("tm", "fo", "fc")
    in_specs = (
        P(rows, None),
        P(rows, None, None),
        P(None, ("fo", "fc")),
        P(),
        P("tm"),
    )
    out_specs = P(rows, None)
    return jax.shard_map(
        body, mesh=split_mesh, in_specs=in_specs, out_specs=out_specs, check_vma=False
    )
```

```python
import jax
import jax.numpy as jnp
from jax import lax
from jax.experimental import pallas as pl
from jax.experimental.pallas import tpu as pltpu
from jax.sharding import Mesh
from jax.sharding import PartitionSpec as P

FRAME_TOK = 256
WINDOW = 4


def passed_along(value, axis, steps):
    count = lax.axis_size(axis)
    initial, last = (max(0, -steps), min(count, count - steps))
    return lax.ppermute(value, axis, [(source, source + steps) for source in range(initial, last)])


def attention_kernel(flag_ref, qkv_ref, halo_ref, out_ref):
    row_count = qkv_ref.shape[2]
    per_frame = FRAME_TOK // row_count
    frame_count = qkv_ref.shape[0] // per_frame
    score_scale = qkv_ref.shape[3] ** (-0.5)
    outer = out_ref.shape[1]
    inner = out_ref.shape[0] // outer
    has_prev = flag_ref[0] > 0

    def frame_rows(ref, block, plane):
        return ref[pl.ds(block, per_frame), plane].reshape(FRAME_TOK, ref.shape[3])

    for frame in range(frame_count):
        query = frame_rows(qkv_ref, frame * per_frame, 0)
        blocks = []
        for back in range(WINDOW):
            source = frame - (WINDOW - 1) + back
            if source >= 0:
                key = frame_rows(qkv_ref, source * per_frame, 1)
                value = frame_rows(qkv_ref, source * per_frame, 2)
            else:
                block = (source + WINDOW - 1) * per_frame
                key, value = frame_rows(halo_ref, block, 0), frame_rows(halo_ref, block, 1)
            scores = (
                lax.dot_general(
                    query, key, (((1,), (1,)), ((), ())), preferred_element_type=jnp.float32
                )
                * score_scale
            )
            if source < 0:
                scores = jnp.where(has_prev, scores, -1e30)
            blocks.append((scores, value))
        row_max = blocks[0][0].max(axis=1, keepdims=True)
        for scores, _ in blocks[1:]:
            row_max = jnp.maximum(row_max, scores.max(axis=1, keepdims=True))
        weights = [jnp.exp(scores - row_max) for scores, _ in blocks]
        row_sum = weights[0].sum(axis=1, keepdims=True)
        for w in weights[1:]:
            row_sum = row_sum + w.sum(axis=1, keepdims=True)
        inverse = 1.0 / row_sum
        total = None
        for w, (_, value) in zip(weights, blocks):
            probability = (w * inverse).astype(jnp.bfloat16)
            part = jnp.dot(probability, value, preferred_element_type=jnp.float32)
            total = part if total is None else total + part
        total = total.astype(out_ref.dtype)
        for piece in range(per_frame):
            row_outer, row_inner = divmod(frame * per_frame + piece, inner)
            rows = total[piece * row_count : (piece + 1) * row_count]
            for dest_outer in range(outer):
                out_ref[dest_outer * inner + row_inner, row_outer] = rows


def attend(flag, qkv, halo, outer, inner):
    row_count, width = qkv.shape[2], qkv.shape[3]
    vmem = pl.BlockSpec(memory_space=pltpu.VMEM)
    return pl.pallas_call(
        attention_kernel,
        out_shape=jax.ShapeDtypeStruct((outer * inner, outer, row_count, width), jnp.bfloat16),
        in_specs=[pl.BlockSpec(memory_space=pltpu.SMEM), vmem, vmem],
        out_specs=vmem,
    )(flag, qkv, halo)


def chunk_kernel(rows_ref, out_ref):
    width = out_ref.shape[3]
    for head in range(out_ref.shape[0]):
        out_ref[head] = rows_ref[:, :, head * width : (head + 1) * width]


def head_chunks(planes, heads):
    lanes, row_count, features = planes.shape
    vmem = pl.BlockSpec(memory_space=pltpu.VMEM)
    return pl.pallas_call(
        chunk_kernel,
        out_shape=jax.ShapeDtypeStruct((heads, lanes, row_count, features // heads), planes.dtype),
        in_specs=[vmem],
        out_specs=vmem,
    )(planes)


def projection_kernel(gathered_ref, weight_ref, out_ref):
    heads, head_dim = gathered_ref.shape[0], gathered_ref.shape[3]
    total = None
    for head in range(heads):
        part = lax.dot_general(
            gathered_ref[head].reshape(-1, head_dim),
            weight_ref[:, head * head_dim : (head + 1) * head_dim],
            (((1,), (1,)), ((), ())),
            preferred_element_type=jnp.float32,
        )
        total = part if total is None else total + part
    out_ref[...] = total.astype(out_ref.dtype)


def project(gathered, weight_t):
    vmem = pl.BlockSpec(memory_space=pltpu.VMEM)
    return pl.pallas_call(
        projection_kernel,
        out_shape=jax.ShapeDtypeStruct(
            (gathered.shape[1] * gathered.shape[2], weight_t.shape[0]), jnp.bfloat16
        ),
        in_specs=[vmem, vmem],
        out_specs=vmem,
    )(gathered, weight_t)


def body(latents, projected, out_weight, gate_table, timesteps):
    row_count = latents.shape[0]
    outer = lax.axis_size("fo")
    inner = lax.axis_size("fc")
    heads = outer * inner
    per_frame = FRAME_TOK // row_count
    shard = lax.axis_index("fo") * inner + lax.axis_index("fc")

    columns = lax.all_gather(out_weight, "fc", axis=1, tiled=True)

    chunks = head_chunks(jnp.transpose(projected, (1, 0, 2)), heads)
    qkv = lax.all_to_all(chunks, ("fo", "fc"), split_axis=0, concat_axis=0, tiled=True)
    halo = passed_along(qkv[per_frame:, 1:3], "tm", 1)
    halo, columns = lax.optimization_barrier((halo, columns))
    flag = (lax.axis_index("tm") > 0).astype(jnp.int32).reshape(1)
    spread = attend(flag, qkv, halo, outer, inner)

    gathered = lax.all_to_all(spread, ("fo", "fc"), split_axis=0, concat_axis=0, tiled=True)
    total = project(gathered, jnp.transpose(columns))
    total = total.reshape(outer, row_count, total.shape[1])
    returned = lax.all_to_all(total, "fo", split_axis=0, concat_axis=0, tiled=True)
    branch = jnp.transpose(returned, (1, 0, 2)).reshape(row_count, -1)

    frame_index = (shard * row_count) // FRAME_TOK
    gate_row = gate_table[timesteps[frame_index]]
    updated = latents.astype(jnp.float32) + gate_row[None, :] * branch.astype(jnp.float32)
    return updated.astype(jnp.bfloat16)


def solution(mesh):
    tm_size, fsdp_size = mesh.devices.shape
    split_mesh = Mesh(mesh.devices.reshape(tm_size, fsdp_size // 2, 2), ("tm", "fo", "fc"))
    rows = ("tm", "fo", "fc")
    in_specs = (
        P(rows, None),
        P(rows, None, None),
        P(None, ("fo", "fc")),
        P(),
        P("tm"),
    )
    out_specs = P(rows, None)
    return jax.shard_map(
        body, mesh=split_mesh, in_specs=in_specs, out_specs=out_specs, check_vma=False
    )
```

```python
import jax
import jax.numpy as jnp
from jax import lax
from jax.experimental import pallas as pl
from jax.experimental.pallas import tpu as pltpu
from jax.sharding import Mesh
from jax.sharding import PartitionSpec as P

FRAME_TOK = 256
WINDOW = 4


def passed_along(value, axis, steps):
    count = lax.axis_size(axis)
    initial, last = (max(0, -steps), min(count, count - steps))
    return lax.ppermute(value, axis, [(source, source + steps) for source in range(initial, last)])


def attention_kernel(flag_ref, q_ref, kv_ref, halo_ref, out_ref):
    qkv_ref = kv_ref
    row_count = qkv_ref.shape[2]
    per_frame = FRAME_TOK // row_count
    frame_count = qkv_ref.shape[0] // per_frame
    score_scale = qkv_ref.shape[3] ** (-0.5)
    inner = out_ref.shape[0] // frame_count
    has_prev = flag_ref[0] > 0

    def frame_rows(ref, block, plane):
        return ref[pl.ds(block, per_frame), plane].reshape(FRAME_TOK, ref.shape[3])

    for frame in range(frame_count):
        query = frame_rows(q_ref, frame * per_frame, 0)
        blocks = []
        for back in range(WINDOW):
            source = frame - (WINDOW - 1) + back
            if source >= 0:
                key = frame_rows(kv_ref, source * per_frame, 0)
                value = frame_rows(kv_ref, source * per_frame, 1)
            else:
                block = (source + WINDOW - 1) * per_frame
                key, value = frame_rows(halo_ref, block, 0), frame_rows(halo_ref, block, 1)
            scores = (
                lax.dot_general(
                    query, key, (((1,), (1,)), ((), ())), preferred_element_type=jnp.float32
                )
                * score_scale
            )
            if source < 0:
                scores = jnp.where(has_prev, scores, -1e30)
            blocks.append((scores, value))
        row_max = blocks[0][0].max(axis=1, keepdims=True)
        for scores, _ in blocks[1:]:
            row_max = jnp.maximum(row_max, scores.max(axis=1, keepdims=True))
        weights = [jnp.exp(scores - row_max) for scores, _ in blocks]
        row_sum = weights[0].sum(axis=1, keepdims=True)
        for w in weights[1:]:
            row_sum = row_sum + w.sum(axis=1, keepdims=True)
        inverse = 1.0 / row_sum
        total = None
        for w, (_, value) in zip(weights, blocks):
            probability = (w * inverse).astype(jnp.bfloat16)
            part = jnp.dot(probability, value, preferred_element_type=jnp.float32)
            total = part if total is None else total + part
        total = total.astype(out_ref.dtype)
        for dest in range(frame * inner, (frame + 1) * inner):
            out_ref[dest] = total


def attend(flag, q, kv, halo, outer, inner):
    width = kv.shape[3]
    vmem = pl.BlockSpec(memory_space=pltpu.VMEM)
    return pl.pallas_call(
        attention_kernel,
        out_shape=jax.ShapeDtypeStruct((outer * inner, FRAME_TOK, width), jnp.bfloat16),
        in_specs=[pl.BlockSpec(memory_space=pltpu.SMEM), vmem, vmem, vmem],
        out_specs=vmem,
    )(flag, q, kv, halo)


def chunk_kernel(rows_ref, query_ref, key_value_ref):
    width = query_ref.shape[3]
    for head in range(query_ref.shape[0]):
        columns = pl.ds(head * width, width)
        query_ref[head] = rows_ref[0:1, :, columns]
        key_value_ref[head] = rows_ref[1:3, :, columns]


def head_chunks(planes, heads):
    lanes, row_count, features = planes.shape
    vmem = pl.BlockSpec(memory_space=pltpu.VMEM)
    return pl.pallas_call(
        chunk_kernel,
        out_shape=(
            jax.ShapeDtypeStruct((heads, 1, row_count, features // heads), planes.dtype),
            jax.ShapeDtypeStruct((heads, lanes - 1, row_count, features // heads), planes.dtype),
        ),
        in_specs=[vmem],
        out_specs=(vmem, vmem),
    )(planes)


def projection_kernel(gathered_ref, weight_ref, out_ref):
    heads, head_dim = gathered_ref.shape[0], gathered_ref.shape[2]
    total = None
    for head in range(heads):
        part = lax.dot_general(
            gathered_ref[head],
            weight_ref[:, head * head_dim : (head + 1) * head_dim],
            (((1,), (1,)), ((), ())),
            preferred_element_type=jnp.float32,
        )
        total = part if total is None else total + part
    out_ref[...] = total.astype(out_ref.dtype)


def project(gathered, weight_t):
    vmem = pl.BlockSpec(memory_space=pltpu.VMEM)
    return pl.pallas_call(
        projection_kernel,
        out_shape=jax.ShapeDtypeStruct((gathered.shape[1], weight_t.shape[0]), jnp.bfloat16),
        in_specs=[vmem, vmem],
        out_specs=vmem,
    )(gathered, weight_t)


def body(latents, projected, out_weight, gate_table, timesteps):
    row_count = latents.shape[0]
    outer = lax.axis_size("fy")
    inner = lax.axis_size("fp")
    heads = outer * inner
    per_frame = FRAME_TOK // row_count
    shard = lax.axis_index("fy") * inner + lax.axis_index("fp")

    columns = lax.all_gather(out_weight, "fy", axis=1, tiled=True)

    query_chunks, key_value_chunks = head_chunks(jnp.transpose(projected, (1, 0, 2)), heads)
    kv = lax.all_to_all(key_value_chunks, ("fy", "fp"), split_axis=0, concat_axis=0, tiled=True)
    halo = passed_along(kv[per_frame:], "tm", 1)
    q = lax.all_to_all(query_chunks, ("fy", "fp"), split_axis=0, concat_axis=0, tiled=True)
    flag = (lax.axis_index("tm") > 0).astype(jnp.int32).reshape(1)
    spread = attend(flag, q, kv, halo, outer, inner)

    gathered = lax.all_to_all(spread, ("fy", "fp"), split_axis=0, concat_axis=0, tiled=True)
    total = project(gathered, jnp.transpose(columns))
    total = total.reshape(inner, row_count, total.shape[1])
    returned = lax.all_to_all(total, "fp", split_axis=0, concat_axis=0, tiled=True)
    width = out_weight.shape[1]
    branch = returned.reshape(inner, row_count, outer, width)
    branch = jnp.transpose(branch, (1, 2, 0, 3)).reshape(row_count, -1)

    frame_index = (shard * row_count) // FRAME_TOK
    gate_row = gate_table[timesteps[frame_index]]
    updated = latents.astype(jnp.float32) + gate_row[None, :] * branch.astype(jnp.float32)
    return updated.astype(jnp.bfloat16)


def solution(mesh):
    tm_size, fsdp_size = mesh.devices.shape
    split_mesh = Mesh(mesh.devices.reshape(tm_size, fsdp_size // 4, 4), ("tm", "fy", "fp"))
    rows = ("tm", "fy", "fp")
    in_specs = (
        P(rows, None),
        P(rows, None, None),
        P(None, ("fy", "fp")),
        P(),
        P("tm"),
    )
    out_specs = P(rows, None)
    return jax.shard_map(
        body, mesh=split_mesh, in_specs=in_specs, out_specs=out_specs, check_vma=False
    )
```

```python
import jax
import jax.numpy as jnp
from jax import lax
from jax.experimental import pallas as pl
from jax.experimental.pallas import tpu as pltpu
from jax.sharding import Mesh
from jax.sharding import PartitionSpec as P

FRAME_TOK = 256
WINDOW = 4


def passed_along(value, axis, steps):
    count = lax.axis_size(axis)
    initial, last = (max(0, -steps), min(count, count - steps))
    return lax.ppermute(value, axis, [(source, source + steps) for source in range(initial, last)])


def attention_kernel(flag_ref, qkv_ref, halo_ref, out_ref):
    row_count = qkv_ref.shape[2]
    per_frame = FRAME_TOK // row_count
    frame_count = qkv_ref.shape[0] // per_frame
    score_scale = qkv_ref.shape[3] ** (-0.5)
    inner = out_ref.shape[0] // frame_count
    has_prev = flag_ref[0] > 0

    def frame_rows(ref, block, plane):
        return ref[pl.ds(block, per_frame), plane].reshape(FRAME_TOK, ref.shape[3])

    for frame in range(frame_count):
        query = frame_rows(qkv_ref, frame * per_frame, 0)
        blocks = []
        for back in range(WINDOW):
            source = frame - (WINDOW - 1) + back
            if source >= 0:
                key = frame_rows(qkv_ref, source * per_frame, 1)
                value = frame_rows(qkv_ref, source * per_frame, 2)
            else:
                block = (source + WINDOW - 1) * per_frame
                key, value = frame_rows(halo_ref, block, 0), frame_rows(halo_ref, block, 1)
            scores = (
                lax.dot_general(
                    query, key, (((1,), (1,)), ((), ())), preferred_element_type=jnp.float32
                )
                * score_scale
            )
            if source < 0:
                scores = jnp.where(has_prev, scores, -1e30)
            blocks.append((scores, value))
        row_max = blocks[0][0].max(axis=1, keepdims=True)
        for scores, _ in blocks[1:]:
            row_max = jnp.maximum(row_max, scores.max(axis=1, keepdims=True))
        weights = [jnp.exp(scores - row_max) for scores, _ in blocks]
        row_sum = weights[0].sum(axis=1, keepdims=True)
        for w in weights[1:]:
            row_sum = row_sum + w.sum(axis=1, keepdims=True)
        inverse = 1.0 / row_sum
        total = None
        for w, (_, value) in zip(weights, blocks):
            probability = (w * inverse).astype(jnp.bfloat16)
            part = jnp.dot(probability, value, preferred_element_type=jnp.float32)
            total = part if total is None else total + part
        total = total.astype(out_ref.dtype)
        for dest in range(frame * inner, (frame + 1) * inner):
            out_ref[dest] = total


def attend(flag, qkv, halo, outer, inner):
    width = qkv.shape[3]
    vmem = pl.BlockSpec(memory_space=pltpu.VMEM)
    return pl.pallas_call(
        attention_kernel,
        out_shape=jax.ShapeDtypeStruct((outer * inner, FRAME_TOK, width), jnp.bfloat16),
        in_specs=[pl.BlockSpec(memory_space=pltpu.SMEM), vmem, vmem],
        out_specs=vmem,
    )(flag, qkv, halo)


def chunk_kernel(rows_ref, out_ref):
    width = out_ref.shape[3]
    for head in range(out_ref.shape[0]):
        out_ref[head] = rows_ref[:, :, head * width : (head + 1) * width]


def head_chunks(planes, heads):
    lanes, row_count, features = planes.shape
    vmem = pl.BlockSpec(memory_space=pltpu.VMEM)
    return pl.pallas_call(
        chunk_kernel,
        out_shape=jax.ShapeDtypeStruct((heads, lanes, row_count, features // heads), planes.dtype),
        in_specs=[vmem],
        out_specs=vmem,
    )(planes)


def projection_kernel(gathered_ref, weight_ref, out_ref, total_ref):
    head = pl.program_id(0)
    part = lax.dot_general(
        gathered_ref[0], weight_ref[...], (((1,), (1,)), ((), ())), preferred_element_type=jnp.float32
    )

    @pl.when(head == 0)
    def _():
        total_ref[...] = part

    @pl.when(head > 0)
    def _():
        total_ref[...] += part

    @pl.when(head == pl.num_programs(0) - 1)
    def _():
        out_ref[...] = total_ref[...].astype(out_ref.dtype)


def project(gathered, weight_t):
    heads, rows, head_dim = gathered.shape
    width = weight_t.shape[0]
    return pl.pallas_call(
        projection_kernel,
        out_shape=jax.ShapeDtypeStruct((rows, width), jnp.bfloat16),
        grid=(heads,),
        in_specs=[
            pl.BlockSpec((1, rows, head_dim), lambda h: (h, 0, 0)),
            pl.BlockSpec((width, head_dim), lambda h: (0, h)),
        ],
        out_specs=pl.BlockSpec((rows, width), lambda h: (0, 0)),
        scratch_shapes=[pltpu.VMEM((rows, width), jnp.float32)],
    )(gathered, weight_t)


def finish_kernel(returned_ref, latents_ref, gate_ref, out_ref):
    senders, _, width = returned_ref.shape
    blocks = gate_ref.shape[1] // (senders * senders)
    for sender in range(senders):
        for block in range(width // blocks):
            column = blocks * (senders * block + sender)
            branch = returned_ref[sender, :, block * blocks : (block + 1) * blocks]
            residual = latents_ref[:, column : column + blocks].astype(jnp.float32)
            gate = gate_ref[:, column : column + blocks]
            out_ref[:, column : column + blocks] = (
                residual + gate * branch.astype(jnp.float32)
            ).astype(out_ref.dtype)


def finish(returned, latents, gate_row):
    vmem = pl.BlockSpec(memory_space=pltpu.VMEM)
    return pl.pallas_call(
        finish_kernel,
        out_shape=jax.ShapeDtypeStruct(latents.shape, jnp.bfloat16),
        in_specs=[vmem, vmem, vmem],
        out_specs=vmem,
    )(returned, latents, gate_row)


def body(latents, projected, out_weight, gate_table, timesteps):
    row_count = latents.shape[0]
    outer = lax.axis_size("fy")
    inner = lax.axis_size("fp")
    heads = outer * inner
    per_frame = FRAME_TOK // row_count
    shard = lax.axis_index("fy") * inner + lax.axis_index("fp")

    columns = lax.all_gather(out_weight, "fy", axis=1, tiled=True)

    chunks = head_chunks(jnp.transpose(projected, (1, 0, 2)), heads)
    qkv = lax.all_to_all(chunks, ("fy", "fp"), split_axis=0, concat_axis=0, tiled=True)
    halo = passed_along(qkv[per_frame:, 1:3], "tm", 1)
    flag = (lax.axis_index("tm") > 0).astype(jnp.int32).reshape(1)
    spread = attend(flag, qkv, halo, outer, inner)

    gathered = lax.all_to_all(spread, ("fy", "fp"), split_axis=0, concat_axis=0, tiled=True)
    total = project(gathered, jnp.transpose(columns))
    total = total.reshape(inner, row_count, total.shape[1])
    returned = lax.all_to_all(total, "fp", split_axis=0, concat_axis=0, tiled=True)

    frame_index = (shard * row_count) // FRAME_TOK
    gate_row = lax.dynamic_index_in_dim(gate_table, timesteps[frame_index], 0, keepdims=True)
    return finish(returned, latents, gate_row)


def solution(mesh):
    tm_size, fsdp_size = mesh.devices.shape
    split_mesh = Mesh(mesh.devices.reshape(tm_size, fsdp_size // 4, 4), ("tm", "fy", "fp"))
    rows = ("tm", "fy", "fp")
    in_specs = (
        P(rows, None),
        P(rows, None, None),
        P(None, ("fy", "fp")),
        P(),
        P("tm"),
    )
    out_specs = P(rows, None)
    return jax.shard_map(
        body, mesh=split_mesh, in_specs=in_specs, out_specs=out_specs, check_vma=False
    )
```

```python
import jax
import jax.numpy as jnp
from jax import lax
from jax.experimental import pallas as pl
from jax.experimental.pallas import tpu as pltpu
from jax.sharding import Mesh
from jax.sharding import PartitionSpec as P

FRAME_TOK = 256
WINDOW = 4


def passed_along(value, axis, steps):
    count = lax.axis_size(axis)
    initial, last = (max(0, -steps), min(count, count - steps))
    return lax.ppermute(value, axis, [(source, source + steps) for source in range(initial, last)])


def attention_kernel(flag_ref, qkv_ref, halo_ref, out_ref):
    row_count = qkv_ref.shape[2]
    per_frame = FRAME_TOK // row_count
    frame_count = qkv_ref.shape[0] // per_frame
    score_scale = qkv_ref.shape[3] ** (-0.5)
    inner = out_ref.shape[0] // frame_count
    has_prev = flag_ref[0] > 0

    def frame_rows(ref, block, plane):
        return ref[pl.ds(block, per_frame), plane].reshape(FRAME_TOK, ref.shape[3])

    for frame in range(frame_count):
        query = frame_rows(qkv_ref, frame * per_frame, 0)
        blocks = []
        for back in range(WINDOW):
            source = frame - (WINDOW - 1) + back
            if source >= 0:
                key = frame_rows(qkv_ref, source * per_frame, 1)
                value = frame_rows(qkv_ref, source * per_frame, 2)
            else:
                block = (source + WINDOW - 1) * per_frame
                key, value = frame_rows(halo_ref, block, 0), frame_rows(halo_ref, block, 1)
            scores = (
                lax.dot_general(
                    query, key, (((1,), (1,)), ((), ())), preferred_element_type=jnp.float32
                )
                * score_scale
            )
            if source < 0:
                scores = jnp.where(has_prev, scores, -1e30)
            blocks.append((scores, value))
        row_max = blocks[0][0].max(axis=1, keepdims=True)
        for scores, _ in blocks[1:]:
            row_max = jnp.maximum(row_max, scores.max(axis=1, keepdims=True))
        weights = [jnp.exp(scores - row_max) for scores, _ in blocks]
        row_sum = weights[0].sum(axis=1, keepdims=True)
        for w in weights[1:]:
            row_sum = row_sum + w.sum(axis=1, keepdims=True)
        inverse = 1.0 / row_sum
        total = None
        for w, (_, value) in zip(weights, blocks):
            probability = (w * inverse).astype(jnp.bfloat16)
            part = jnp.dot(probability, value, preferred_element_type=jnp.float32)
            total = part if total is None else total + part
        total = total.astype(out_ref.dtype)
        for dest in range(frame * inner, (frame + 1) * inner):
            out_ref[dest] = total


def attend(flag, qkv, halo, outer, inner):
    width = qkv.shape[3]
    vmem = pl.BlockSpec(memory_space=pltpu.VMEM)
    return pl.pallas_call(
        attention_kernel,
        out_shape=jax.ShapeDtypeStruct((outer * inner, FRAME_TOK, width), jnp.bfloat16),
        in_specs=[pl.BlockSpec(memory_space=pltpu.SMEM), vmem, vmem],
        out_specs=vmem,
    )(flag, qkv, halo)


def chunk_kernel(rows_ref, out_ref):
    width = out_ref.shape[3]
    for head in range(out_ref.shape[0]):
        out_ref[head] = rows_ref[:, :, head * width : (head + 1) * width]


def head_chunks(planes, heads):
    lanes, row_count, features = planes.shape
    vmem = pl.BlockSpec(memory_space=pltpu.VMEM)
    return pl.pallas_call(
        chunk_kernel,
        out_shape=jax.ShapeDtypeStruct((heads, lanes, row_count, features // heads), planes.dtype),
        in_specs=[vmem],
        out_specs=vmem,
    )(planes)


def projection_kernel(gathered_ref, weight_ref, out_ref):
    heads, head_dim = gathered_ref.shape[0], gathered_ref.shape[2]
    total = None
    for head in range(heads):
        part = lax.dot_general(
            gathered_ref[head],
            weight_ref[:, head * head_dim : (head + 1) * head_dim],
            (((1,), (1,)), ((), ())),
            preferred_element_type=jnp.float32,
        )
        total = part if total is None else total + part
    out_ref[...] = total.astype(out_ref.dtype)


def project(gathered, weight_t):
    heads, rows, head_dim = gathered.shape
    width, depth = weight_t.shape
    step = 128
    return pl.pallas_call(
        projection_kernel,
        out_shape=jax.ShapeDtypeStruct((rows, width), jnp.bfloat16),
        grid=(width // step,),
        in_specs=[
            pl.BlockSpec((heads, rows, head_dim), lambda n: (0, 0, 0)),
            pl.BlockSpec((step, depth), lambda n: (n, 0)),
        ],
        out_specs=pl.BlockSpec((rows, step), lambda n: (0, n)),
    )(gathered, weight_t)


def finish_kernel(returned_ref, latents_ref, gate_ref, out_ref):
    senders, _, width = returned_ref.shape
    blocks = gate_ref.shape[1] // (senders * senders)
    for sender in range(senders):
        for block in range(width // blocks):
            column = blocks * (senders * block + sender)
            branch = returned_ref[sender, :, block * blocks : (block + 1) * blocks]
            residual = latents_ref[:, column : column + blocks].astype(jnp.float32)
            gate = gate_ref[:, column : column + blocks]
            out_ref[:, column : column + blocks] = (
                residual + gate * branch.astype(jnp.float32)
            ).astype(out_ref.dtype)


def finish(returned, latents, gate_row):
    vmem = pl.BlockSpec(memory_space=pltpu.VMEM)
    return pl.pallas_call(
        finish_kernel,
        out_shape=jax.ShapeDtypeStruct(latents.shape, jnp.bfloat16),
        in_specs=[vmem, vmem, vmem],
        out_specs=vmem,
    )(returned, latents, gate_row)


def body(latents, projected, out_weight, gate_table, timesteps):
    row_count = latents.shape[0]
    outer = lax.axis_size("fy")
    inner = lax.axis_size("fp")
    heads = outer * inner
    per_frame = FRAME_TOK // row_count
    shard = lax.axis_index("fy") * inner + lax.axis_index("fp")

    columns = lax.all_gather(out_weight, "fy", axis=1, tiled=True)

    chunks = head_chunks(jnp.transpose(projected, (1, 0, 2)), heads)
    qkv = lax.all_to_all(chunks, ("fy", "fp"), split_axis=0, concat_axis=0, tiled=True)
    halo = passed_along(qkv[per_frame:, 1:3], "tm", 1)
    flag = (lax.axis_index("tm") > 0).astype(jnp.int32).reshape(1)
    spread = attend(flag, qkv, halo, outer, inner)

    gathered = lax.all_to_all(spread, ("fy", "fp"), split_axis=0, concat_axis=0, tiled=True)
    total = project(gathered, jnp.transpose(columns))
    total = total.reshape(inner, row_count, total.shape[1])
    returned = lax.all_to_all(total, "fp", split_axis=0, concat_axis=0, tiled=True)

    frame_index = (shard * row_count) // FRAME_TOK
    gate_row = lax.dynamic_index_in_dim(gate_table, timesteps[frame_index], 0, keepdims=True)
    return finish(returned, latents, gate_row)


def solution(mesh):
    tm_size, fsdp_size = mesh.devices.shape
    split_mesh = Mesh(mesh.devices.reshape(tm_size, fsdp_size // 4, 4), ("tm", "fy", "fp"))
    rows = ("tm", "fy", "fp")
    in_specs = (
        P(rows, None),
        P(rows, None, None),
        P(None, ("fy", "fp")),
        P(),
        P("tm"),
    )
    out_specs = P(rows, None)
    return jax.shard_map(
        body, mesh=split_mesh, in_specs=in_specs, out_specs=out_specs, check_vma=False
    )
```

```python
import jax
import jax.numpy as jnp
from jax import lax
from jax.experimental import pallas as pl
from jax.experimental.pallas import tpu as pltpu
from jax.sharding import Mesh
from jax.sharding import PartitionSpec as P

FRAME_TOK = 256
WINDOW = 4


def passed_along(value, axis, steps):
    count = lax.axis_size(axis)
    initial, last = (max(0, -steps), min(count, count - steps))
    return lax.ppermute(value, axis, [(source, source + steps) for source in range(initial, last)])


def attention_kernel(flag_ref, qkv_ref, halo_ref, out_ref):
    row_count = qkv_ref.shape[2]
    per_frame = FRAME_TOK // row_count
    frame_count = qkv_ref.shape[0] // per_frame
    score_scale = qkv_ref.shape[3] ** (-0.5)
    inner = out_ref.shape[0] // frame_count
    has_prev = flag_ref[0] > 0

    def frame_rows(ref, block, plane):
        return ref[pl.ds(block, per_frame), plane].reshape(FRAME_TOK, ref.shape[3])

    for frame in range(frame_count):
        query = frame_rows(qkv_ref, frame * per_frame, 0)
        blocks = []
        for back in range(WINDOW):
            source = frame - (WINDOW - 1) + back
            if source >= 0:
                key = frame_rows(qkv_ref, source * per_frame, 1)
                value = frame_rows(qkv_ref, source * per_frame, 2)
            else:
                block = (source + WINDOW - 1) * per_frame
                key, value = frame_rows(halo_ref, block, 0), frame_rows(halo_ref, block, 1)
            scores = (
                lax.dot_general(
                    query, key, (((1,), (1,)), ((), ())), preferred_element_type=jnp.float32
                )
                * score_scale
            )
            if source < 0:
                scores = jnp.where(has_prev, scores, -1e30)
            blocks.append((scores, value))
        row_max = blocks[0][0].max(axis=1, keepdims=True)
        for scores, _ in blocks[1:]:
            row_max = jnp.maximum(row_max, scores.max(axis=1, keepdims=True))
        weights = [jnp.exp(scores - row_max) for scores, _ in blocks]
        row_sum = weights[0].sum(axis=1, keepdims=True)
        for w in weights[1:]:
            row_sum = row_sum + w.sum(axis=1, keepdims=True)
        inverse = 1.0 / row_sum
        total = None
        for w, (_, value) in zip(weights, blocks):
            probability = (w * inverse).astype(jnp.bfloat16)
            part = jnp.dot(probability, value, preferred_element_type=jnp.float32)
            total = part if total is None else total + part
        total = total.astype(out_ref.dtype)
        for dest in range(frame * inner, (frame + 1) * inner):
            out_ref[dest] = total


def attend(flag, qkv, halo, outer, inner):
    width = qkv.shape[3]
    vmem = pl.BlockSpec(memory_space=pltpu.VMEM)
    return pl.pallas_call(
        attention_kernel,
        out_shape=jax.ShapeDtypeStruct((outer * inner, FRAME_TOK, width), jnp.bfloat16),
        in_specs=[pl.BlockSpec(memory_space=pltpu.SMEM), vmem, vmem],
        out_specs=vmem,
    )(flag, qkv, halo)


def chunk_kernel(rows_ref, out_ref):
    width = out_ref.shape[3]
    for head in range(out_ref.shape[0]):
        out_ref[head] = rows_ref[:, :, head * width : (head + 1) * width]


def head_chunks(planes, heads):
    lanes, row_count, features = planes.shape
    vmem = pl.BlockSpec(memory_space=pltpu.VMEM)
    return pl.pallas_call(
        chunk_kernel,
        out_shape=jax.ShapeDtypeStruct((heads, lanes, row_count, features // heads), planes.dtype),
        in_specs=[vmem],
        out_specs=vmem,
    )(planes)


def projection_kernel(gathered_ref, weight_ref, out_ref):
    heads, head_dim = gathered_ref.shape[0], gathered_ref.shape[2]
    total = None
    for head in range(heads):
        part = lax.dot_general(
            gathered_ref[head],
            weight_ref[:, head * head_dim : (head + 1) * head_dim],
            (((1,), (1,)), ((), ())),
            preferred_element_type=jnp.float32,
        )
        total = part if total is None else total + part
    out_ref[...] = total.astype(out_ref.dtype)


def project(gathered, weight_t):
    vmem = pl.BlockSpec(memory_space=pltpu.VMEM)
    return pl.pallas_call(
        projection_kernel,
        out_shape=jax.ShapeDtypeStruct((gathered.shape[1], weight_t.shape[0]), jnp.bfloat16),
        in_specs=[vmem, vmem],
        out_specs=vmem,
    )(gathered, weight_t)


def finish_kernel(returned_ref, latents_ref, gate_ref, out_ref):
    senders, _, width = returned_ref.shape
    blocks = gate_ref.shape[1] // (senders * senders)
    for sender in range(senders):
        for block in range(width // blocks):
            column = blocks * (senders * block + sender)
            branch = returned_ref[sender, :, block * blocks : (block + 1) * blocks]
            residual = latents_ref[:, column : column + blocks].astype(jnp.float32)
            gate = gate_ref[:, column : column + blocks]
            out_ref[:, column : column + blocks] = (
                residual + gate * branch.astype(jnp.float32)
            ).astype(out_ref.dtype)


def finish(returned, latents, gate_row):
    vmem = pl.BlockSpec(memory_space=pltpu.VMEM)
    return pl.pallas_call(
        finish_kernel,
        out_shape=jax.ShapeDtypeStruct(latents.shape, jnp.bfloat16),
        in_specs=[vmem, vmem, vmem],
        out_specs=vmem,
    )(returned, latents, gate_row)


def body(latents, projected, out_weight, gate_table, timesteps):
    row_count = latents.shape[0]
    outer = lax.axis_size("fy")
    inner = lax.axis_size("fp")
    heads = outer * inner
    per_frame = FRAME_TOK // row_count
    shard = lax.axis_index("fy") * inner + lax.axis_index("fp")

    chunks = head_chunks(jnp.transpose(projected, (1, 0, 2)), heads)
    qkv = lax.all_to_all(chunks, ("fy", "fp"), split_axis=0, concat_axis=0, tiled=True)
    qkv, own_weight = lax.optimization_barrier((qkv, out_weight))
    shards = [own_weight]
    for shift in range(1, outer):
        pairs = [(source, (source + shift) % outer) for source in range(outer)]
        shards.append(lax.ppermute(own_weight, "fy", pairs))
    me_outer = lax.axis_index("fy")
    order = (me_outer - jnp.arange(outer, dtype=jnp.int32)) % outer
    columns = jnp.stack(shards)[order]
    columns = jnp.transpose(columns, (1, 0, 2)).reshape(out_weight.shape[0], -1)
    halo = passed_along(qkv[per_frame:, 1:3], "tm", 1)
    flag = (lax.axis_index("tm") > 0).astype(jnp.int32).reshape(1)
    spread = attend(flag, qkv, halo, outer, inner)

    gathered = lax.all_to_all(spread, ("fy", "fp"), split_axis=0, concat_axis=0, tiled=True)
    total = project(gathered, jnp.transpose(columns))
    total = total.reshape(inner, row_count, total.shape[1])
    returned = lax.all_to_all(total, "fp", split_axis=0, concat_axis=0, tiled=True)

    frame_index = (shard * row_count) // FRAME_TOK
    gate_row = lax.dynamic_index_in_dim(gate_table, timesteps[frame_index], 0, keepdims=True)
    return finish(returned, latents, gate_row)


def solution(mesh):
    tm_size, fsdp_size = mesh.devices.shape
    split_mesh = Mesh(mesh.devices.reshape(tm_size, fsdp_size // 4, 4), ("tm", "fy", "fp"))
    rows = ("tm", "fy", "fp")
    in_specs = (
        P(rows, None),
        P(rows, None, None),
        P(None, ("fy", "fp")),
        P(),
        P("tm"),
    )
    out_specs = P(rows, None)
    return jax.shard_map(
        body, mesh=split_mesh, in_specs=in_specs, out_specs=out_specs, check_vma=False
    )
```

```python
import jax
import jax.numpy as jnp
from jax import lax
from jax.experimental import pallas as pl
from jax.experimental.pallas import tpu as pltpu
from jax.sharding import Mesh
from jax.sharding import PartitionSpec as P

FRAME_TOK = 256
WINDOW = 4


def passed_along(value, axis, steps):
    count = lax.axis_size(axis)
    initial, last = (max(0, -steps), min(count, count - steps))
    return lax.ppermute(value, axis, [(source, source + steps) for source in range(initial, last)])


def attention_kernel(flag_ref, qkv_ref, halo_ref, out_ref):
    row_count = qkv_ref.shape[2]
    per_frame = FRAME_TOK // row_count
    frame_count = qkv_ref.shape[0] // per_frame
    score_scale = qkv_ref.shape[3] ** (-0.5)
    inner = out_ref.shape[0] // frame_count
    has_prev = flag_ref[0] > 0

    def frame_rows(ref, block, plane):
        return ref[pl.ds(block, per_frame), plane].reshape(FRAME_TOK, ref.shape[3])

    for frame in range(frame_count):
        query = frame_rows(qkv_ref, frame * per_frame, 0)
        blocks = []
        for back in range(WINDOW):
            source = frame - (WINDOW - 1) + back
            if source >= 0:
                key = frame_rows(qkv_ref, source * per_frame, 1)
                value = frame_rows(qkv_ref, source * per_frame, 2)
            else:
                block = (source + WINDOW - 1) * per_frame
                key, value = frame_rows(halo_ref, block, 0), frame_rows(halo_ref, block, 1)
            scores = (
                lax.dot_general(
                    query, key, (((1,), (1,)), ((), ())), preferred_element_type=jnp.float32
                )
                * score_scale
            )
            if source < 0:
                scores = jnp.where(has_prev, scores, -1e30)
            blocks.append((scores, value))
        row_max = blocks[0][0].max(axis=1, keepdims=True)
        for scores, _ in blocks[1:]:
            row_max = jnp.maximum(row_max, scores.max(axis=1, keepdims=True))
        weights = [jnp.exp(scores - row_max) for scores, _ in blocks]
        row_sum = weights[0].sum(axis=1, keepdims=True)
        for w in weights[1:]:
            row_sum = row_sum + w.sum(axis=1, keepdims=True)
        inverse = 1.0 / row_sum
        total = None
        for w, (_, value) in zip(weights, blocks):
            probability = (w * inverse).astype(jnp.bfloat16)
            part = jnp.dot(probability, value, preferred_element_type=jnp.float32)
            total = part if total is None else total + part
        total = total.astype(out_ref.dtype)
        for dest in range(frame * inner, (frame + 1) * inner):
            out_ref[dest] = total


def attend(flag, qkv, halo, outer, inner):
    width = qkv.shape[3]
    vmem = pl.BlockSpec(memory_space=pltpu.VMEM)
    return pl.pallas_call(
        attention_kernel,
        out_shape=jax.ShapeDtypeStruct((outer * inner, FRAME_TOK, width), jnp.bfloat16),
        in_specs=[pl.BlockSpec(memory_space=pltpu.SMEM), vmem, vmem],
        out_specs=vmem,
    )(flag, qkv, halo)


def chunk_kernel(rows_ref, out_ref):
    width = out_ref.shape[3]
    for head in range(out_ref.shape[0]):
        out_ref[head] = rows_ref[:, :, head * width : (head + 1) * width]


def head_chunks(planes, heads):
    lanes, row_count, features = planes.shape
    vmem = pl.BlockSpec(memory_space=pltpu.VMEM)
    return pl.pallas_call(
        chunk_kernel,
        out_shape=jax.ShapeDtypeStruct((heads, lanes, row_count, features // heads), planes.dtype),
        in_specs=[vmem],
        out_specs=vmem,
    )(planes)


def projection_kernel(place_ref, gathered_ref, *refs):
    weight_refs, out_ref = refs[:-1], refs[-1]
    heads, head_dim = gathered_ref.shape[0], gathered_ref.shape[2]
    for shift, weight_ref in enumerate(weight_refs):
        total = None
        for head in range(heads):
            part = lax.dot_general(
                gathered_ref[head],
                weight_ref[:, head * head_dim : (head + 1) * head_dim],
                (((1,), (1,)), ((), ())),
                preferred_element_type=jnp.float32,
            )
            total = part if total is None else total + part
        total = total.astype(out_ref.dtype)
        rows = out_ref.shape[2]
        for group in range(out_ref.shape[0]):
            out_ref[group, place_ref[shift]] = total[group * rows : (group + 1) * rows]


def project(place, gathered, weights_t, groups):
    vmem = pl.BlockSpec(memory_space=pltpu.VMEM)
    count, width = len(weights_t), weights_t[0].shape[0]
    rows = gathered.shape[1] // groups
    return pl.pallas_call(
        projection_kernel,
        out_shape=jax.ShapeDtypeStruct((groups, count, rows, width), jnp.bfloat16),
        in_specs=[pl.BlockSpec(memory_space=pltpu.SMEM)] + [vmem] * (count + 1),
        out_specs=vmem,
    )(place, gathered, *weights_t)


def finish_kernel(returned_ref, latents_ref, gate_ref, out_ref):
    senders, blocks, _, width = returned_ref.shape
    for block in range(blocks):
        for sender in range(senders):
            column = width * (senders * block + sender)
            branch = returned_ref[sender, block]
            residual = latents_ref[:, column : column + width].astype(jnp.float32)
            gate = gate_ref[:, column : column + width]
            out_ref[:, column : column + width] = (
                residual + gate * branch.astype(jnp.float32)
            ).astype(out_ref.dtype)


def finish(returned, latents, gate_row):
    vmem = pl.BlockSpec(memory_space=pltpu.VMEM)
    return pl.pallas_call(
        finish_kernel,
        out_shape=jax.ShapeDtypeStruct(latents.shape, jnp.bfloat16),
        in_specs=[vmem, vmem, vmem],
        out_specs=vmem,
    )(returned, latents, gate_row)


def body(latents, projected, out_weight, gate_table, timesteps):
    row_count = latents.shape[0]
    outer = lax.axis_size("fy")
    inner = lax.axis_size("fp")
    heads = outer * inner
    per_frame = FRAME_TOK // row_count
    shard = lax.axis_index("fy") * inner + lax.axis_index("fp")

    chunks = head_chunks(jnp.transpose(projected, (1, 0, 2)), heads)
    qkv = lax.all_to_all(chunks, ("fy", "fp"), split_axis=0, concat_axis=0, tiled=True)
    qkv, own_weight = lax.optimization_barrier((qkv, out_weight))
    shards = [own_weight]
    for shift in range(1, outer):
        pairs = [(source, (source + shift) % outer) for source in range(outer)]
        shards.append(lax.ppermute(own_weight, "fy", pairs))
    me_outer = lax.axis_index("fy")
    place = ((me_outer - jnp.arange(outer, dtype=jnp.int32)) % outer).astype(jnp.int32)
    halo = passed_along(qkv[per_frame:, 1:3], "tm", 1)
    flag = (lax.axis_index("tm") > 0).astype(jnp.int32).reshape(1)
    spread = attend(flag, qkv, halo, outer, inner)

    gathered = lax.all_to_all(spread, ("fy", "fp"), split_axis=0, concat_axis=0, tiled=True)
    total = project(place, gathered, [jnp.transpose(shard_w) for shard_w in shards], inner)
    returned = lax.all_to_all(total, "fp", split_axis=0, concat_axis=0, tiled=True)

    frame_index = (shard * row_count) // FRAME_TOK
    gate_row = lax.dynamic_index_in_dim(gate_table, timesteps[frame_index], 0, keepdims=True)
    return finish(returned, latents, gate_row)


def solution(mesh):
    tm_size, fsdp_size = mesh.devices.shape
    split_mesh = Mesh(mesh.devices.reshape(tm_size, fsdp_size // 4, 4), ("tm", "fy", "fp"))
    rows = ("tm", "fy", "fp")
    in_specs = (
        P(rows, None),
        P(rows, None, None),
        P(None, ("fy", "fp")),
        P(),
        P("tm"),
    )
    out_specs = P(rows, None)
    return jax.shard_map(
        body, mesh=split_mesh, in_specs=in_specs, out_specs=out_specs, check_vma=False
    )
```

```python
import jax
import jax.numpy as jnp
from jax import lax
from jax.experimental import pallas as pl
from jax.experimental.pallas import tpu as pltpu
from jax.sharding import Mesh
from jax.sharding import PartitionSpec as P

FRAME_TOK = 256
WINDOW = 4


def passed_along(value, axis, steps):
    count = lax.axis_size(axis)
    initial, last = (max(0, -steps), min(count, count - steps))
    return lax.ppermute(value, axis, [(source, source + steps) for source in range(initial, last)])


def attention_kernel(flag_ref, qkv_ref, halo_ref, out_ref):
    row_count = qkv_ref.shape[2]
    per_frame = FRAME_TOK // row_count
    frame_count = qkv_ref.shape[0] // per_frame
    score_scale = qkv_ref.shape[3] ** (-0.5)
    inner = out_ref.shape[0] // frame_count
    has_prev = flag_ref[0] > 0

    def frame_rows(ref, block, plane):
        return ref[pl.ds(block, per_frame), plane].reshape(FRAME_TOK, ref.shape[3])

    for frame in range(frame_count):
        query = frame_rows(qkv_ref, frame * per_frame, 0)
        blocks = []
        for back in range(WINDOW):
            source = frame - (WINDOW - 1) + back
            if source >= 0:
                key = frame_rows(qkv_ref, source * per_frame, 1)
                value = frame_rows(qkv_ref, source * per_frame, 2)
            else:
                block = (source + WINDOW - 1) * per_frame
                key, value = frame_rows(halo_ref, block, 0), frame_rows(halo_ref, block, 1)
            scores = (
                lax.dot_general(
                    query, key, (((1,), (1,)), ((), ())), preferred_element_type=jnp.float32
                )
                * score_scale
            )
            if source < 0:
                scores = jnp.where(has_prev, scores, -1e30)
            blocks.append((scores, value))
        row_max = blocks[0][0].max(axis=1, keepdims=True)
        for scores, _ in blocks[1:]:
            row_max = jnp.maximum(row_max, scores.max(axis=1, keepdims=True))
        weights = [jnp.exp(scores - row_max) for scores, _ in blocks]
        row_sum = weights[0].sum(axis=1, keepdims=True)
        for w in weights[1:]:
            row_sum = row_sum + w.sum(axis=1, keepdims=True)
        inverse = 1.0 / row_sum
        total = None
        for w, (_, value) in zip(weights, blocks):
            probability = (w * inverse).astype(jnp.bfloat16)
            part = jnp.dot(probability, value, preferred_element_type=jnp.float32)
            total = part if total is None else total + part
        total = total.astype(out_ref.dtype)
        for dest in range(frame * inner, (frame + 1) * inner):
            out_ref[dest] = total


def attend(flag, qkv, halo, outer, inner):
    width = qkv.shape[3]
    vmem = pl.BlockSpec(memory_space=pltpu.VMEM)
    return pl.pallas_call(
        attention_kernel,
        out_shape=jax.ShapeDtypeStruct((outer * inner, FRAME_TOK, width), jnp.bfloat16),
        in_specs=[pl.BlockSpec(memory_space=pltpu.SMEM), vmem, vmem],
        out_specs=vmem,
    )(flag, qkv, halo)


def chunk_kernel(rows_ref, out_ref):
    width = out_ref.shape[3]
    for head in range(out_ref.shape[0]):
        out_ref[head] = rows_ref[:, :, head * width : (head + 1) * width]


def head_chunks(planes, heads):
    lanes, row_count, features = planes.shape
    vmem = pl.BlockSpec(memory_space=pltpu.VMEM)
    return pl.pallas_call(
        chunk_kernel,
        out_shape=jax.ShapeDtypeStruct((heads, lanes, row_count, features // heads), planes.dtype),
        in_specs=[vmem],
        out_specs=vmem,
    )(planes)


def projection_kernel(place_ref, gathered_ref, *refs):
    weight_refs, out_ref = refs[:-1], refs[-1]
    heads, head_dim = gathered_ref.shape[0], gathered_ref.shape[2]
    for shift, weight_ref in enumerate(weight_refs):
        total = None
        for head in range(heads):
            part = lax.dot_general(
                gathered_ref[head],
                weight_ref[:, head * head_dim : (head + 1) * head_dim],
                (((1,), (1,)), ((), ())),
                preferred_element_type=jnp.float32,
            )
            total = part if total is None else total + part
        total = total.astype(out_ref.dtype)
        rows = out_ref.shape[2]
        for group in range(out_ref.shape[0]):
            out_ref[group, place_ref[shift]] = total[group * rows : (group + 1) * rows]


def project(place, gathered, weights_t, groups):
    vmem = pl.BlockSpec(memory_space=pltpu.VMEM)
    count, width = len(weights_t), weights_t[0].shape[0]
    rows = gathered.shape[1] // groups
    return pl.pallas_call(
        projection_kernel,
        out_shape=jax.ShapeDtypeStruct((groups, count, rows, width), jnp.bfloat16),
        in_specs=[pl.BlockSpec(memory_space=pltpu.SMEM)] + [vmem] * (count + 1),
        out_specs=vmem,
    )(place, gathered, *weights_t)


def finish_kernel(returned_ref, latents_ref, gate_ref, out_ref):
    senders, blocks, _, width = returned_ref.shape
    for block in range(blocks):
        for sender in range(senders):
            column = width * (senders * block + sender)
            branch = returned_ref[sender, block]
            residual = latents_ref[:, column : column + width].astype(jnp.float32)
            gate = gate_ref[:, column : column + width]
            out_ref[:, column : column + width] = (
                residual + gate * branch.astype(jnp.float32)
            ).astype(out_ref.dtype)


def finish(returned, latents, gate_row):
    vmem = pl.BlockSpec(memory_space=pltpu.VMEM)
    return pl.pallas_call(
        finish_kernel,
        out_shape=jax.ShapeDtypeStruct(latents.shape, jnp.bfloat16),
        in_specs=[vmem, vmem, vmem],
        out_specs=vmem,
    )(returned, latents, gate_row)


def body(latents, projected, out_weight, gate_table, timesteps):
    row_count = latents.shape[0]
    outer = lax.axis_size("fy")
    inner = lax.axis_size("fp")
    heads = outer * inner
    per_frame = FRAME_TOK // row_count
    shard = lax.axis_index("fy") * inner + lax.axis_index("fp")

    chunks = head_chunks(jnp.transpose(projected, (1, 0, 2)), heads)
    qkv = lax.all_to_all(chunks, ("fy", "fp"), split_axis=0, concat_axis=0, tiled=True)
    qkv, own_weight = lax.optimization_barrier((qkv, out_weight))
    shards = [own_weight]
    for shift in range(1, outer):
        pairs = [(source, (source + shift) % outer) for source in range(outer)]
        shards.append(lax.ppermute(own_weight, "fy", pairs))
    me_outer = lax.axis_index("fy")
    place = ((me_outer - jnp.arange(outer, dtype=jnp.int32)) % outer).astype(jnp.int32)
    halo = passed_along(qkv[per_frame:, 1:3], "tm", 1)
    flag = (lax.axis_index("tm") > 0).astype(jnp.int32).reshape(1)
    spread = attend(flag, qkv, halo, outer, inner)
    spread, *shards = lax.optimization_barrier((spread, *shards))

    gathered = lax.all_to_all(spread, ("fy", "fp"), split_axis=0, concat_axis=0, tiled=True)
    total = project(place, gathered, [jnp.transpose(shard_w) for shard_w in shards], inner)
    returned = lax.all_to_all(total, "fp", split_axis=0, concat_axis=0, tiled=True)

    frame_index = (shard * row_count) // FRAME_TOK
    gate_row = lax.dynamic_index_in_dim(gate_table, timesteps[frame_index], 0, keepdims=True)
    return finish(returned, latents, gate_row)


def solution(mesh):
    tm_size, fsdp_size = mesh.devices.shape
    split_mesh = Mesh(mesh.devices.reshape(tm_size, fsdp_size // 4, 4), ("tm", "fy", "fp"))
    rows = ("tm", "fy", "fp")
    in_specs = (
        P(rows, None),
        P(rows, None, None),
        P(None, ("fy", "fp")),
        P(),
        P("tm"),
    )
    out_specs = P(rows, None)
    return jax.shard_map(
        body, mesh=split_mesh, in_specs=in_specs, out_specs=out_specs, check_vma=False
    )
```

```python
import jax
import jax.numpy as jnp
from jax import lax
from jax.experimental import pallas as pl
from jax.experimental.pallas import tpu as pltpu
from jax.sharding import Mesh
from jax.sharding import PartitionSpec as P

FRAME_TOK = 256
WINDOW = 4


def passed_along(value, axis, steps):
    count = lax.axis_size(axis)
    initial, last = (max(0, -steps), min(count, count - steps))
    return lax.ppermute(value, axis, [(source, source + steps) for source in range(initial, last)])


def attention_kernel(flag_ref, qkv_ref, halo_ref, out_ref):
    row_count = qkv_ref.shape[2]
    per_frame = FRAME_TOK // row_count
    frame_count = qkv_ref.shape[0] // per_frame
    score_scale = qkv_ref.shape[3] ** (-0.5)
    inner = out_ref.shape[0] // frame_count
    has_prev = flag_ref[0] > 0

    def frame_rows(ref, block, plane):
        return ref[pl.ds(block, per_frame), plane].reshape(FRAME_TOK, ref.shape[3])

    for frame in range(frame_count):
        query = frame_rows(qkv_ref, frame * per_frame, 0)
        blocks = []
        for back in range(WINDOW):
            source = frame - (WINDOW - 1) + back
            if source >= 0:
                key = frame_rows(qkv_ref, source * per_frame, 1)
                value = frame_rows(qkv_ref, source * per_frame, 2)
            else:
                block = (source + WINDOW - 1) * per_frame
                key, value = frame_rows(halo_ref, block, 0), frame_rows(halo_ref, block, 1)
            scores = (
                lax.dot_general(
                    query, key, (((1,), (1,)), ((), ())), preferred_element_type=jnp.float32
                )
                * score_scale
            )
            if source < 0:
                scores = jnp.where(has_prev, scores, -1e30)
            blocks.append((scores, value))
        row_max = blocks[0][0].max(axis=1, keepdims=True)
        for scores, _ in blocks[1:]:
            row_max = jnp.maximum(row_max, scores.max(axis=1, keepdims=True))
        weights = [jnp.exp(scores - row_max) for scores, _ in blocks]
        row_sum = weights[0].sum(axis=1, keepdims=True)
        for w in weights[1:]:
            row_sum = row_sum + w.sum(axis=1, keepdims=True)
        inverse = 1.0 / row_sum
        total = None
        for w, (_, value) in zip(weights, blocks):
            probability = (w * inverse).astype(jnp.bfloat16)
            part = jnp.dot(probability, value, preferred_element_type=jnp.float32)
            total = part if total is None else total + part
        total = total.astype(out_ref.dtype)
        for dest in range(frame * inner, (frame + 1) * inner):
            out_ref[dest] = total


def attend(flag, qkv, halo, outer, inner):
    width = qkv.shape[3]
    vmem = pl.BlockSpec(memory_space=pltpu.VMEM)
    return pl.pallas_call(
        attention_kernel,
        out_shape=jax.ShapeDtypeStruct((outer * inner, FRAME_TOK, width), jnp.bfloat16),
        in_specs=[pl.BlockSpec(memory_space=pltpu.SMEM), vmem, vmem],
        out_specs=vmem,
    )(flag, qkv, halo)


def chunk_kernel(rows_ref, out_ref):
    width = out_ref.shape[3]
    for head in range(out_ref.shape[0]):
        out_ref[head] = rows_ref[:, :, head * width : (head + 1) * width]


def head_chunks(planes, heads):
    lanes, row_count, features = planes.shape
    vmem = pl.BlockSpec(memory_space=pltpu.VMEM)
    return pl.pallas_call(
        chunk_kernel,
        out_shape=jax.ShapeDtypeStruct((heads, lanes, row_count, features // heads), planes.dtype),
        in_specs=[vmem],
        out_specs=vmem,
    )(planes)


def projection_kernel(place_ref, gathered_ref, *refs):
    weight_refs, out_ref = refs[:-1], refs[-1]
    heads, head_dim = gathered_ref.shape[0], gathered_ref.shape[2]
    for shift, weight_ref in enumerate(weight_refs):
        total = None
        for head in range(heads):
            part = lax.dot_general(
                gathered_ref[head],
                weight_ref[:, head * head_dim : (head + 1) * head_dim],
                (((1,), (1,)), ((), ())),
                preferred_element_type=jnp.float32,
            )
            total = part if total is None else total + part
        total = total.astype(out_ref.dtype)
        rows = out_ref.shape[2]
        for group in range(out_ref.shape[0]):
            out_ref[group, place_ref[shift]] = total[group * rows : (group + 1) * rows]


def project(place, gathered, weights_t, groups):
    vmem = pl.BlockSpec(memory_space=pltpu.VMEM)
    count, width = len(weights_t), weights_t[0].shape[0]
    rows = gathered.shape[1] // groups
    return pl.pallas_call(
        projection_kernel,
        out_shape=jax.ShapeDtypeStruct((groups, count, rows, width), jnp.bfloat16),
        in_specs=[pl.BlockSpec(memory_space=pltpu.SMEM)] + [vmem] * (count + 1),
        out_specs=vmem,
    )(place, gathered, *weights_t)


def finish_kernel(returned_ref, latents_ref, gate_ref, out_ref):
    senders, blocks, _, width = returned_ref.shape
    for block in range(blocks):
        for sender in range(senders):
            column = width * (senders * block + sender)
            branch = returned_ref[sender, block]
            residual = latents_ref[:, column : column + width].astype(jnp.float32)
            gate = gate_ref[:, column : column + width]
            out_ref[:, column : column + width] = (
                residual + gate * branch.astype(jnp.float32)
            ).astype(out_ref.dtype)


def finish(returned, latents, gate_row):
    vmem = pl.BlockSpec(memory_space=pltpu.VMEM)
    return pl.pallas_call(
        finish_kernel,
        out_shape=jax.ShapeDtypeStruct(latents.shape, jnp.bfloat16),
        in_specs=[vmem, vmem, vmem],
        out_specs=vmem,
    )(returned, latents, gate_row)


def body(latents, projected, out_weight, gate_table, timesteps):
    row_count = latents.shape[0]
    outer = lax.axis_size("fy")
    inner = lax.axis_size("fp")
    heads = outer * inner
    per_frame = FRAME_TOK // row_count
    shard = lax.axis_index("fy") * inner + lax.axis_index("fp")

    chunks = head_chunks(jnp.transpose(projected, (1, 0, 2)), heads)
    qkv = lax.all_to_all(chunks, ("fy", "fp"), split_axis=0, concat_axis=0, tiled=True)
    own_weight = out_weight
    shards = [own_weight]
    for shift in range(1, outer):
        pairs = [(source, (source + shift) % outer) for source in range(outer)]
        shards.append(lax.ppermute(own_weight, "fy", pairs))
    me_outer = lax.axis_index("fy")
    place = ((me_outer - jnp.arange(outer, dtype=jnp.int32)) % outer).astype(jnp.int32)
    halo = passed_along(qkv[per_frame:, 1:3], "tm", 1)
    flag = (lax.axis_index("tm") > 0).astype(jnp.int32).reshape(1)
    spread = attend(flag, qkv, halo, outer, inner)
    spread, *shards = lax.optimization_barrier((spread, *shards))

    gathered = lax.all_to_all(spread, ("fy", "fp"), split_axis=0, concat_axis=0, tiled=True)
    total = project(place, gathered, [jnp.transpose(shard_w) for shard_w in shards], inner)
    returned = lax.all_to_all(total, "fp", split_axis=0, concat_axis=0, tiled=True)

    frame_index = (shard * row_count) // FRAME_TOK
    gate_row = lax.dynamic_index_in_dim(gate_table, timesteps[frame_index], 0, keepdims=True)
    return finish(returned, latents, gate_row)


def solution(mesh):
    tm_size, fsdp_size = mesh.devices.shape
    split_mesh = Mesh(mesh.devices.reshape(tm_size, fsdp_size // 4, 4), ("tm", "fy", "fp"))
    rows = ("tm", "fy", "fp")
    in_specs = (
        P(rows, None),
        P(rows, None, None),
        P(None, ("fy", "fp")),
        P(),
        P("tm"),
    )
    out_specs = P(rows, None)
    return jax.shard_map(
        body, mesh=split_mesh, in_specs=in_specs, out_specs=out_specs, check_vma=False
    )
```

```python
import jax
import jax.numpy as jnp
from jax import lax
from jax.experimental import pallas as pl
from jax.experimental.pallas import tpu as pltpu
from jax.sharding import Mesh
from jax.sharding import PartitionSpec as P

FRAME_TOK = 256
WINDOW = 4


def passed_along(value, axis, steps):
    count = lax.axis_size(axis)
    initial, last = (max(0, -steps), min(count, count - steps))
    return lax.ppermute(value, axis, [(source, source + steps) for source in range(initial, last)])


def attention_kernel(flag_ref, qkv_ref, halo_ref, out_ref):
    row_count = qkv_ref.shape[2]
    per_frame = FRAME_TOK // row_count
    frame_count = qkv_ref.shape[0] // per_frame
    score_scale = qkv_ref.shape[3] ** (-0.5)
    inner = out_ref.shape[0] // frame_count
    has_prev = flag_ref[0] > 0

    def frame_rows(ref, block, plane):
        return ref[pl.ds(block, per_frame), plane].reshape(FRAME_TOK, ref.shape[3])

    for frame in range(frame_count):
        query = frame_rows(qkv_ref, frame * per_frame, 0)
        blocks = []
        for back in range(WINDOW):
            source = frame - (WINDOW - 1) + back
            if source >= 0:
                key = frame_rows(qkv_ref, source * per_frame, 1)
                value = frame_rows(qkv_ref, source * per_frame, 2)
            else:
                block = (source + WINDOW - 1) * per_frame
                key, value = frame_rows(halo_ref, block, 0), frame_rows(halo_ref, block, 1)
            scores = (
                lax.dot_general(
                    query, key, (((1,), (1,)), ((), ())), preferred_element_type=jnp.float32
                )
                * score_scale
            )
            if source < 0:
                scores = jnp.where(has_prev, scores, -1e30)
            blocks.append((scores, value))
        row_max = blocks[0][0].max(axis=1, keepdims=True)
        for scores, _ in blocks[1:]:
            row_max = jnp.maximum(row_max, scores.max(axis=1, keepdims=True))
        weights = [jnp.exp(scores - row_max) for scores, _ in blocks]
        row_sum = weights[0].sum(axis=1, keepdims=True)
        for w in weights[1:]:
            row_sum = row_sum + w.sum(axis=1, keepdims=True)
        inverse = 1.0 / row_sum
        total = None
        for w, (_, value) in zip(weights, blocks):
            probability = (w * inverse).astype(jnp.bfloat16)
            part = jnp.dot(probability, value, preferred_element_type=jnp.float32)
            total = part if total is None else total + part
        total = total.astype(out_ref.dtype)
        for dest in range(frame * inner, (frame + 1) * inner):
            out_ref[dest] = total


def attend(flag, qkv, halo, outer, inner):
    width = qkv.shape[3]
    vmem = pl.BlockSpec(memory_space=pltpu.VMEM)
    return pl.pallas_call(
        attention_kernel,
        out_shape=jax.ShapeDtypeStruct((outer * inner, FRAME_TOK, width), jnp.bfloat16),
        in_specs=[pl.BlockSpec(memory_space=pltpu.SMEM), vmem, vmem],
        out_specs=vmem,
    )(flag, qkv, halo)


def chunk_kernel(rows_ref, out_ref):
    width = out_ref.shape[3]
    for head in range(out_ref.shape[0]):
        out_ref[head] = rows_ref[:, :, head * width : (head + 1) * width]


def head_chunks(planes, heads):
    lanes, row_count, features = planes.shape
    vmem = pl.BlockSpec(memory_space=pltpu.VMEM)
    return pl.pallas_call(
        chunk_kernel,
        out_shape=jax.ShapeDtypeStruct((heads, lanes, row_count, features // heads), planes.dtype),
        in_specs=[vmem],
        out_specs=vmem,
    )(planes)


def projection_kernel(place_ref, gathered_ref, *refs):
    weight_refs, out_ref = refs[:-1], refs[-1]
    heads, head_dim = gathered_ref.shape[0], gathered_ref.shape[2]
    rows = out_ref.shape[2]
    slots = out_ref.shape[1]
    pieces = [[ref] for ref in weight_refs[:2]] + [list(weight_refs[2:4])] + [[weight_refs[4]]]
    for shift in range(slots):
        parts = pieces[shift]
        per_part = heads // len(parts)
        total = None
        for head in range(heads):
            weight_ref = parts[head // per_part]
            column = (head % per_part) * head_dim
            part = lax.dot_general(
                gathered_ref[head],
                weight_ref[:, column : column + head_dim],
                (((1,), (1,)), ((), ())),
                preferred_element_type=jnp.float32,
            )
            total = part if total is None else total + part
        total = total.astype(out_ref.dtype)
        for group in range(out_ref.shape[0]):
            out_ref[group, place_ref[shift]] = total[group * rows : (group + 1) * rows]


def project(place, gathered, weights_t, groups):
    vmem = pl.BlockSpec(memory_space=pltpu.VMEM)
    count, width = 4, weights_t[0].shape[0]
    rows = gathered.shape[1] // groups
    return pl.pallas_call(
        projection_kernel,
        out_shape=jax.ShapeDtypeStruct((groups, count, rows, width), jnp.bfloat16),
        in_specs=[pl.BlockSpec(memory_space=pltpu.SMEM)] + [vmem] * (len(weights_t) + 1),
        out_specs=vmem,
    )(place, gathered, *weights_t)


def finish_kernel(returned_ref, latents_ref, gate_ref, out_ref):
    senders, blocks, _, width = returned_ref.shape
    for block in range(blocks):
        for sender in range(senders):
            column = width * (senders * block + sender)
            branch = returned_ref[sender, block]
            residual = latents_ref[:, column : column + width].astype(jnp.float32)
            gate = gate_ref[:, column : column + width]
            out_ref[:, column : column + width] = (
                residual + gate * branch.astype(jnp.float32)
            ).astype(out_ref.dtype)


def finish(returned, latents, gate_row):
    vmem = pl.BlockSpec(memory_space=pltpu.VMEM)
    return pl.pallas_call(
        finish_kernel,
        out_shape=jax.ShapeDtypeStruct(latents.shape, jnp.bfloat16),
        in_specs=[vmem, vmem, vmem],
        out_specs=vmem,
    )(returned, latents, gate_row)


def body(latents, projected, out_weight, gate_table, timesteps):
    row_count = latents.shape[0]
    outer = lax.axis_size("fy")
    inner = lax.axis_size("fp")
    heads = outer * inner
    per_frame = FRAME_TOK // row_count
    shard = lax.axis_index("fy") * inner + lax.axis_index("fp")

    chunks = head_chunks(jnp.transpose(projected, (1, 0, 2)), heads)
    qkv = lax.all_to_all(chunks, ("fy", "fp"), split_axis=0, concat_axis=0, tiled=True)
    def shifted(value, shift):
        pairs = [(source, (source + shift) % outer) for source in range(outer)]
        return lax.ppermute(value, "fy", pairs)

    half = out_weight.shape[0] // 2
    from_below = shifted(out_weight, 1)
    from_above = shifted(out_weight, -1)
    far_low = shifted(from_below[:half], 1)
    far_high = shifted(from_above[half:], -1)
    shards = [out_weight, from_below, (far_low, far_high), from_above]
    me_outer = lax.axis_index("fy")
    place = ((me_outer - jnp.arange(outer, dtype=jnp.int32)) % outer).astype(jnp.int32)
    halo = passed_along(qkv[per_frame:, 1:3], "tm", 1)
    flag = (lax.axis_index("tm") > 0).astype(jnp.int32).reshape(1)
    spread = attend(flag, qkv, halo, outer, inner)
    spread, shards = lax.optimization_barrier((spread, shards))

    gathered = lax.all_to_all(spread, ("fy", "fp"), split_axis=0, concat_axis=0, tiled=True)
    flat = [shards[0], shards[1], shards[2][0], shards[2][1], shards[3]]
    total = project(place, gathered, [jnp.transpose(shard_w) for shard_w in flat], inner)
    returned = lax.all_to_all(total, "fp", split_axis=0, concat_axis=0, tiled=True)

    frame_index = (shard * row_count) // FRAME_TOK
    gate_row = lax.dynamic_index_in_dim(gate_table, timesteps[frame_index], 0, keepdims=True)
    return finish(returned, latents, gate_row)


def solution(mesh):
    tm_size, fsdp_size = mesh.devices.shape
    split_mesh = Mesh(mesh.devices.reshape(tm_size, fsdp_size // 4, 4), ("tm", "fy", "fp"))
    rows = ("tm", "fy", "fp")
    in_specs = (
        P(rows, None),
        P(rows, None, None),
        P(None, ("fy", "fp")),
        P(),
        P("tm"),
    )
    out_specs = P(rows, None)
    return jax.shard_map(
        body, mesh=split_mesh, in_specs=in_specs, out_specs=out_specs, check_vma=False
    )
```

```python
import jax
import jax.numpy as jnp
from jax import lax
from jax.experimental import pallas as pl
from jax.experimental.pallas import tpu as pltpu
from jax.sharding import Mesh
from jax.sharding import PartitionSpec as P

FRAME_TOK = 256
WINDOW = 4


def passed_along(value, axis, steps):
    count = lax.axis_size(axis)
    initial, last = (max(0, -steps), min(count, count - steps))
    return lax.ppermute(value, axis, [(source, source + steps) for source in range(initial, last)])


def attention_kernel(flag_ref, qkv_ref, halo_ref, out_ref):
    row_count = qkv_ref.shape[2]
    per_frame = FRAME_TOK // row_count
    frame_count = qkv_ref.shape[0] // per_frame
    score_scale = qkv_ref.shape[3] ** (-0.5)
    inner = out_ref.shape[0] // frame_count
    has_prev = flag_ref[0] > 0

    def frame_rows(ref, block, plane):
        return ref[pl.ds(block, per_frame), plane].reshape(FRAME_TOK, ref.shape[3])

    for frame in range(frame_count):
        query = frame_rows(qkv_ref, frame * per_frame, 0)
        blocks = []
        for back in range(WINDOW):
            source = frame - (WINDOW - 1) + back
            if source >= 0:
                key = frame_rows(qkv_ref, source * per_frame, 1)
                value = frame_rows(qkv_ref, source * per_frame, 2)
            else:
                block = (source + WINDOW - 1) * per_frame
                key, value = frame_rows(halo_ref, block, 0), frame_rows(halo_ref, block, 1)
            scores = (
                lax.dot_general(
                    query, key, (((1,), (1,)), ((), ())), preferred_element_type=jnp.float32
                )
                * score_scale
            )
            if source < 0:
                scores = jnp.where(has_prev, scores, -1e30)
            blocks.append((scores, value))
        row_max = blocks[0][0].max(axis=1, keepdims=True)
        for scores, _ in blocks[1:]:
            row_max = jnp.maximum(row_max, scores.max(axis=1, keepdims=True))
        weights = [jnp.exp(scores - row_max) for scores, _ in blocks]
        row_sum = weights[0].sum(axis=1, keepdims=True)
        for w in weights[1:]:
            row_sum = row_sum + w.sum(axis=1, keepdims=True)
        inverse = 1.0 / row_sum
        total = None
        for w, (_, value) in zip(weights, blocks):
            probability = (w * inverse).astype(jnp.bfloat16)
            part = jnp.dot(probability, value, preferred_element_type=jnp.float32)
            total = part if total is None else total + part
        total = total.astype(out_ref.dtype)
        for dest in range(frame * inner, (frame + 1) * inner):
            out_ref[dest] = total


def attend(flag, qkv, halo, outer, inner):
    width = qkv.shape[3]
    vmem = pl.BlockSpec(memory_space=pltpu.VMEM)
    return pl.pallas_call(
        attention_kernel,
        out_shape=jax.ShapeDtypeStruct((outer * inner, FRAME_TOK, width), jnp.bfloat16),
        in_specs=[pl.BlockSpec(memory_space=pltpu.SMEM), vmem, vmem],
        out_specs=vmem,
    )(flag, qkv, halo)


def chunk_kernel(rows_ref, out_ref):
    width = out_ref.shape[3]
    for head in range(out_ref.shape[0]):
        out_ref[head] = rows_ref[:, :, head * width : (head + 1) * width]


def head_chunks(planes, heads):
    lanes, row_count, features = planes.shape
    vmem = pl.BlockSpec(memory_space=pltpu.VMEM)
    return pl.pallas_call(
        chunk_kernel,
        out_shape=jax.ShapeDtypeStruct((heads, lanes, row_count, features // heads), planes.dtype),
        in_specs=[vmem],
        out_specs=vmem,
    )(planes)


def projection_kernel(place_ref, gathered_ref, *refs):
    weight_refs, out_ref = refs[:-1], refs[-1]
    heads, head_dim = gathered_ref.shape[0], gathered_ref.shape[2]
    rows = out_ref.shape[2]
    slots = out_ref.shape[1]
    pieces = [[ref] for ref in weight_refs[:2]] + [list(weight_refs[2:4])] + [[weight_refs[4]]]
    for shift in range(slots):
        parts = pieces[shift]
        per_part = heads // len(parts)
        total = None
        for head in range(heads):
            weight_ref = parts[head // per_part]
            column = (head % per_part) * head_dim
            part = lax.dot_general(
                gathered_ref[head],
                weight_ref[:, column : column + head_dim],
                (((1,), (1,)), ((), ())),
                preferred_element_type=jnp.float32,
            )
            total = part if total is None else total + part
        total = total.astype(out_ref.dtype)
        for group in range(out_ref.shape[0]):
            out_ref[group, place_ref[shift]] = total[group * rows : (group + 1) * rows]


def project(place, gathered, weights_t, groups):
    vmem = pl.BlockSpec(memory_space=pltpu.VMEM)
    count, width = 4, weights_t[0].shape[0]
    rows = gathered.shape[1] // groups
    return pl.pallas_call(
        projection_kernel,
        out_shape=jax.ShapeDtypeStruct((groups, count, rows, width), jnp.bfloat16),
        in_specs=[pl.BlockSpec(memory_space=pltpu.SMEM)] + [vmem] * (len(weights_t) + 1),
        out_specs=vmem,
    )(place, gathered, *weights_t)


def finish_kernel(returned_ref, latents_ref, gate_ref, out_ref):
    senders, blocks, _, width = returned_ref.shape
    for block in range(blocks):
        for sender in range(senders):
            column = width * (senders * block + sender)
            branch = returned_ref[sender, block]
            residual = latents_ref[:, column : column + width].astype(jnp.float32)
            gate = gate_ref[:, column : column + width]
            out_ref[:, column : column + width] = (
                residual + gate * branch.astype(jnp.float32)
            ).astype(out_ref.dtype)


def finish(returned, latents, gate_row):
    vmem = pl.BlockSpec(memory_space=pltpu.VMEM)
    return pl.pallas_call(
        finish_kernel,
        out_shape=jax.ShapeDtypeStruct(latents.shape, jnp.bfloat16),
        in_specs=[vmem, vmem, vmem],
        out_specs=vmem,
    )(returned, latents, gate_row)


def body(latents, projected, out_weight, gate_table, timesteps):
    row_count = latents.shape[0]
    outer = lax.axis_size("fy")
    inner = lax.axis_size("fp")
    heads = outer * inner
    per_frame = FRAME_TOK // row_count
    shard = lax.axis_index("fy") * inner + lax.axis_index("fp")

    chunks = head_chunks(jnp.transpose(projected, (1, 0, 2)), heads)
    qkv = lax.all_to_all(chunks, ("fy", "fp"), split_axis=0, concat_axis=0, tiled=True)
    def shifted(value, shift):
        pairs = [(source, (source + shift) % outer) for source in range(outer)]
        return lax.ppermute(value, "fy", pairs)

    half = out_weight.shape[0] // 2
    from_below = shifted(out_weight, 1)
    from_above = shifted(out_weight, -1)
    far_low = shifted(from_below[:half], 1)
    far_high = shifted(from_above[half:], -1)
    shards = [out_weight, from_below, (far_low, far_high), from_above]
    me_outer = lax.axis_index("fy")
    place = ((me_outer - jnp.arange(outer, dtype=jnp.int32)) % outer).astype(jnp.int32)
    halo = passed_along(qkv[per_frame:, 1:3], "tm", 1)
    flag = (lax.axis_index("tm") > 0).astype(jnp.int32).reshape(1)
    spread = attend(flag, qkv, halo, outer, inner)
    spread, near = lax.optimization_barrier((spread, (shards[1], shards[3])))
    shards = [shards[0], near[0], shards[2], near[1]]

    gathered = lax.all_to_all(spread, ("fy", "fp"), split_axis=0, concat_axis=0, tiled=True)
    flat = [shards[0], shards[1], shards[2][0], shards[2][1], shards[3]]
    total = project(place, gathered, [jnp.transpose(shard_w) for shard_w in flat], inner)
    returned = lax.all_to_all(total, "fp", split_axis=0, concat_axis=0, tiled=True)

    frame_index = (shard * row_count) // FRAME_TOK
    gate_row = lax.dynamic_index_in_dim(gate_table, timesteps[frame_index], 0, keepdims=True)
    return finish(returned, latents, gate_row)


def solution(mesh):
    tm_size, fsdp_size = mesh.devices.shape
    split_mesh = Mesh(mesh.devices.reshape(tm_size, fsdp_size // 4, 4), ("tm", "fy", "fp"))
    rows = ("tm", "fy", "fp")
    in_specs = (
        P(rows, None),
        P(rows, None, None),
        P(None, ("fy", "fp")),
        P(),
        P("tm"),
    )
    out_specs = P(rows, None)
    return jax.shard_map(
        body, mesh=split_mesh, in_specs=in_specs, out_specs=out_specs, check_vma=False
    )
```

```python
import jax
import jax.numpy as jnp
from jax import lax
from jax.experimental import pallas as pl
from jax.experimental.pallas import tpu as pltpu
from jax.sharding import Mesh
from jax.sharding import PartitionSpec as P

FRAME_TOK = 256
WINDOW = 4


def passed_along(value, axis, steps):
    count = lax.axis_size(axis)
    initial, last = (max(0, -steps), min(count, count - steps))
    return lax.ppermute(value, axis, [(source, source + steps) for source in range(initial, last)])


def attention_kernel(flag_ref, qkv_ref, halo_ref, out_ref):
    row_count = qkv_ref.shape[2]
    per_frame = FRAME_TOK // row_count
    frame_count = qkv_ref.shape[0] // per_frame
    score_scale = qkv_ref.shape[3] ** (-0.5)
    inner = out_ref.shape[0] // frame_count
    has_prev = flag_ref[0] > 0

    def frame_rows(ref, block, plane):
        return ref[pl.ds(block, per_frame), plane].reshape(FRAME_TOK, ref.shape[3])

    for frame in range(frame_count):
        query = frame_rows(qkv_ref, frame * per_frame, 0)
        blocks = []
        for back in range(WINDOW):
            source = frame - (WINDOW - 1) + back
            if source >= 0:
                key = frame_rows(qkv_ref, source * per_frame, 1)
                value = frame_rows(qkv_ref, source * per_frame, 2)
            else:
                block = (source + WINDOW - 1) * per_frame
                key, value = frame_rows(halo_ref, block, 0), frame_rows(halo_ref, block, 1)
            scores = (
                lax.dot_general(
                    query, key, (((1,), (1,)), ((), ())), preferred_element_type=jnp.float32
                )
                * score_scale
            )
            if source < 0:
                scores = jnp.where(has_prev, scores, -1e30)
            blocks.append((scores, value))
        row_max = blocks[0][0].max(axis=1, keepdims=True)
        for scores, _ in blocks[1:]:
            row_max = jnp.maximum(row_max, scores.max(axis=1, keepdims=True))
        weights = [jnp.exp(scores - row_max) for scores, _ in blocks]
        row_sum = weights[0].sum(axis=1, keepdims=True)
        for w in weights[1:]:
            row_sum = row_sum + w.sum(axis=1, keepdims=True)
        inverse = 1.0 / row_sum
        total = None
        for w, (_, value) in zip(weights, blocks):
            probability = (w * inverse).astype(jnp.bfloat16)
            part = jnp.dot(probability, value, preferred_element_type=jnp.float32)
            total = part if total is None else total + part
        total = total.astype(out_ref.dtype)
        for dest in range(frame * inner, (frame + 1) * inner):
            out_ref[dest] = total


def attend(flag, qkv, halo, outer, inner):
    width = qkv.shape[3]
    vmem = pl.BlockSpec(memory_space=pltpu.VMEM)
    return pl.pallas_call(
        attention_kernel,
        out_shape=jax.ShapeDtypeStruct((outer * inner, FRAME_TOK, width), jnp.bfloat16),
        in_specs=[pl.BlockSpec(memory_space=pltpu.SMEM), vmem, vmem],
        out_specs=vmem,
    )(flag, qkv, halo)


def chunk_kernel(rows_ref, out_ref):
    width = out_ref.shape[3]
    for head in range(out_ref.shape[0]):
        out_ref[head] = rows_ref[:, :, head * width : (head + 1) * width]


def head_chunks(planes, heads):
    lanes, row_count, features = planes.shape
    vmem = pl.BlockSpec(memory_space=pltpu.VMEM)
    return pl.pallas_call(
        chunk_kernel,
        out_shape=jax.ShapeDtypeStruct((heads, lanes, row_count, features // heads), planes.dtype),
        in_specs=[vmem],
        out_specs=vmem,
    )(planes)


def projection_kernel(place_ref, gathered_ref, *refs):
    weight_refs, out_ref = refs[:-1], refs[-1]
    heads, head_dim = gathered_ref.shape[0], gathered_ref.shape[2]
    rows = out_ref.shape[2]
    slots = out_ref.shape[1]
    pieces = [[ref] for ref in weight_refs[:2]] + [list(weight_refs[2:4])] + [[weight_refs[4]]]
    for shift in range(slots):
        parts = pieces[shift]
        per_part = heads // len(parts)
        total = None
        for head in range(heads):
            weight_ref = parts[head // per_part]
            column = (head % per_part) * head_dim
            part = lax.dot_general(
                gathered_ref[head],
                weight_ref[:, column : column + head_dim],
                (((1,), (1,)), ((), ())),
                preferred_element_type=jnp.float32,
            )
            total = part if total is None else total + part
        total = total.astype(out_ref.dtype)
        for group in range(out_ref.shape[0]):
            out_ref[group, place_ref[shift]] = total[group * rows : (group + 1) * rows]


def project(place, gathered, weights_t, groups):
    vmem = pl.BlockSpec(memory_space=pltpu.VMEM)
    count, width = 4, weights_t[0].shape[0]
    rows = gathered.shape[1] // groups
    return pl.pallas_call(
        projection_kernel,
        out_shape=jax.ShapeDtypeStruct((groups, count, rows, width), jnp.bfloat16),
        in_specs=[pl.BlockSpec(memory_space=pltpu.SMEM)] + [vmem] * (len(weights_t) + 1),
        out_specs=vmem,
    )(place, gathered, *weights_t)


def finish_kernel(returned_ref, latents_ref, gate_ref, out_ref):
    senders, blocks, _, width = returned_ref.shape
    for block in range(blocks):
        for sender in range(senders):
            column = width * (senders * block + sender)
            branch = returned_ref[sender, block]
            residual = latents_ref[:, column : column + width].astype(jnp.float32)
            gate = gate_ref[:, column : column + width]
            out_ref[:, column : column + width] = (
                residual + gate * branch.astype(jnp.float32)
            ).astype(out_ref.dtype)


def finish(returned, latents, gate_row):
    vmem = pl.BlockSpec(memory_space=pltpu.VMEM)
    return pl.pallas_call(
        finish_kernel,
        out_shape=jax.ShapeDtypeStruct(latents.shape, jnp.bfloat16),
        in_specs=[vmem, vmem, vmem],
        out_specs=vmem,
    )(returned, latents, gate_row)


def body(latents, projected, out_weight, gate_table, timesteps):
    row_count = latents.shape[0]
    outer = lax.axis_size("fy")
    inner = lax.axis_size("fp")
    heads = outer * inner
    per_frame = FRAME_TOK // row_count
    shard = lax.axis_index("fy") * inner + lax.axis_index("fp")

    chunks = head_chunks(jnp.transpose(projected, (1, 0, 2)), heads)
    qkv = lax.all_to_all(chunks, ("fy", "fp"), split_axis=0, concat_axis=0, tiled=True)
    def shifted(value, shift):
        pairs = [(source, (source + shift) % outer) for source in range(outer)]
        return lax.ppermute(value, "fy", pairs)

    half = out_weight.shape[0] // 2
    from_below = shifted(out_weight, 1)
    from_above = shifted(out_weight, -1)
    far_low = shifted(from_below[:half], 1)
    far_high = shifted(from_above[half:], -1)
    shards = [out_weight, from_below, (far_low, far_high), from_above]
    me_outer = lax.axis_index("fy")
    place = ((me_outer - jnp.arange(outer, dtype=jnp.int32)) % outer).astype(jnp.int32)
    halo = passed_along(qkv[per_frame:, 1:3], "tm", 1)
    halo, near = lax.optimization_barrier((halo, (shards[1], shards[3])))
    shards = [shards[0], near[0], shards[2], near[1]]
    flag = (lax.axis_index("tm") > 0).astype(jnp.int32).reshape(1)
    spread = attend(flag, qkv, halo, outer, inner)

    gathered = lax.all_to_all(spread, ("fy", "fp"), split_axis=0, concat_axis=0, tiled=True)
    flat = [shards[0], shards[1], shards[2][0], shards[2][1], shards[3]]
    total = project(place, gathered, [jnp.transpose(shard_w) for shard_w in flat], inner)
    returned = lax.all_to_all(total, "fp", split_axis=0, concat_axis=0, tiled=True)

    frame_index = (shard * row_count) // FRAME_TOK
    gate_row = lax.dynamic_index_in_dim(gate_table, timesteps[frame_index], 0, keepdims=True)
    return finish(returned, latents, gate_row)


def solution(mesh):
    tm_size, fsdp_size = mesh.devices.shape
    split_mesh = Mesh(mesh.devices.reshape(tm_size, fsdp_size // 4, 4), ("tm", "fy", "fp"))
    rows = ("tm", "fy", "fp")
    in_specs = (
        P(rows, None),
        P(rows, None, None),
        P(None, ("fy", "fp")),
        P(),
        P("tm"),
    )
    out_specs = P(rows, None)
    return jax.shard_map(
        body, mesh=split_mesh, in_specs=in_specs, out_specs=out_specs, check_vma=False
    )
```

```python
import jax
import jax.numpy as jnp
from jax import lax
from jax.experimental import pallas as pl
from jax.experimental.pallas import tpu as pltpu
from jax.sharding import Mesh
from jax.sharding import PartitionSpec as P

FRAME_TOK = 256
WINDOW = 4


def passed_along(value, axis, steps):
    count = lax.axis_size(axis)
    initial, last = (max(0, -steps), min(count, count - steps))
    return lax.ppermute(value, axis, [(source, source + steps) for source in range(initial, last)])


def attention_kernel(flag_ref, qkv_ref, halo_ref, out_ref):
    row_count = qkv_ref.shape[2]
    per_frame = FRAME_TOK // row_count
    frame_count = qkv_ref.shape[0] // per_frame
    score_scale = qkv_ref.shape[3] ** (-0.5)
    inner = out_ref.shape[0] // frame_count
    has_prev = flag_ref[0] > 0

    def frame_rows(ref, block, plane):
        return ref[pl.ds(block, per_frame), plane].reshape(FRAME_TOK, ref.shape[3])

    for frame in range(frame_count):
        query = frame_rows(qkv_ref, frame * per_frame, 0)
        blocks = []
        for back in range(WINDOW):
            source = frame - (WINDOW - 1) + back
            if source >= 0:
                key = frame_rows(qkv_ref, source * per_frame, 1)
                value = frame_rows(qkv_ref, source * per_frame, 2)
            else:
                block = (source + WINDOW - 1) * per_frame
                key, value = frame_rows(halo_ref, block, 0), frame_rows(halo_ref, block, 1)
            scores = (
                lax.dot_general(
                    query, key, (((1,), (1,)), ((), ())), preferred_element_type=jnp.float32
                )
                * score_scale
            )
            if source < 0:
                scores = jnp.where(has_prev, scores, -1e30)
            blocks.append((scores, value))
        row_max = blocks[0][0].max(axis=1, keepdims=True)
        for scores, _ in blocks[1:]:
            row_max = jnp.maximum(row_max, scores.max(axis=1, keepdims=True))
        weights = [jnp.exp(scores - row_max) for scores, _ in blocks]
        row_sum = weights[0].sum(axis=1, keepdims=True)
        for w in weights[1:]:
            row_sum = row_sum + w.sum(axis=1, keepdims=True)
        inverse = 1.0 / row_sum
        total = None
        for w, (_, value) in zip(weights, blocks):
            probability = (w * inverse).astype(jnp.bfloat16)
            part = jnp.dot(probability, value, preferred_element_type=jnp.float32)
            total = part if total is None else total + part
        total = total.astype(out_ref.dtype)
        for dest in range(frame * inner, (frame + 1) * inner):
            out_ref[dest] = total


def attend(flag, qkv, halo, outer, inner):
    width = qkv.shape[3]
    vmem = pl.BlockSpec(memory_space=pltpu.VMEM)
    return pl.pallas_call(
        attention_kernel,
        out_shape=jax.ShapeDtypeStruct((outer * inner, FRAME_TOK, width), jnp.bfloat16),
        in_specs=[pl.BlockSpec(memory_space=pltpu.SMEM), vmem, vmem],
        out_specs=vmem,
    )(flag, qkv, halo)


def chunk_kernel(rows_ref, out_ref):
    width = out_ref.shape[3]
    for head in range(out_ref.shape[0]):
        out_ref[head] = rows_ref[:, :, head * width : (head + 1) * width]


def head_chunks(planes, heads):
    lanes, row_count, features = planes.shape
    vmem = pl.BlockSpec(memory_space=pltpu.VMEM)
    return pl.pallas_call(
        chunk_kernel,
        out_shape=jax.ShapeDtypeStruct((heads, lanes, row_count, features // heads), planes.dtype),
        in_specs=[vmem],
        out_specs=vmem,
    )(planes)


def projection_kernel(place_ref, gathered_ref, *refs):
    count = (len(refs) - 2) // 2
    weight_hbm, out_ref = refs[:count], refs[count]
    weight_vmem, semaphores = refs[count + 1 : 2 * count + 1], refs[2 * count + 1]
    copies = [
        pltpu.make_async_copy(weight_hbm[i], weight_vmem[i], semaphores.at[i]) for i in range(count)
    ]
    for copy in copies:
        copy.start()
    heads, head_dim = gathered_ref.shape[0], gathered_ref.shape[2]
    rows = out_ref.shape[2]
    slots = out_ref.shape[1]
    pieces = [[0], [1], [2, 3], [4]]
    for shift in range(slots):
        parts = pieces[shift]
        for index in parts:
            copies[index].wait()
        per_part = heads // len(parts)
        total = None
        for head in range(heads):
            weight_ref = weight_vmem[parts[head // per_part]]
            column = (head % per_part) * head_dim
            part = lax.dot_general(
                gathered_ref[head],
                weight_ref[:, column : column + head_dim],
                (((1,), (1,)), ((), ())),
                preferred_element_type=jnp.float32,
            )
            total = part if total is None else total + part
        total = total.astype(out_ref.dtype)
        for group in range(out_ref.shape[0]):
            out_ref[group, place_ref[shift]] = total[group * rows : (group + 1) * rows]


def project(place, gathered, weights_t, groups):
    vmem = pl.BlockSpec(memory_space=pltpu.VMEM)
    hbm = pl.BlockSpec(memory_space=pl.ANY)
    count, width = 4, weights_t[0].shape[0]
    rows = gathered.shape[1] // groups
    return pl.pallas_call(
        projection_kernel,
        out_shape=jax.ShapeDtypeStruct((groups, count, rows, width), jnp.bfloat16),
        in_specs=[pl.BlockSpec(memory_space=pltpu.SMEM), vmem] + [hbm] * len(weights_t),
        out_specs=vmem,
        scratch_shapes=[pltpu.VMEM(w.shape, w.dtype) for w in weights_t]
        + [pltpu.SemaphoreType.DMA((len(weights_t),))],
    )(place, gathered, *weights_t)


def finish_kernel(returned_ref, latents_ref, gate_ref, out_ref):
    senders, blocks, _, width = returned_ref.shape
    for block in range(blocks):
        for sender in range(senders):
            column = width * (senders * block + sender)
            branch = returned_ref[sender, block]
            residual = latents_ref[:, column : column + width].astype(jnp.float32)
            gate = gate_ref[:, column : column + width]
            out_ref[:, column : column + width] = (
                residual + gate * branch.astype(jnp.float32)
            ).astype(out_ref.dtype)


def finish(returned, latents, gate_row):
    vmem = pl.BlockSpec(memory_space=pltpu.VMEM)
    return pl.pallas_call(
        finish_kernel,
        out_shape=jax.ShapeDtypeStruct(latents.shape, jnp.bfloat16),
        in_specs=[vmem, vmem, vmem],
        out_specs=vmem,
    )(returned, latents, gate_row)


def body(latents, projected, out_weight, gate_table, timesteps):
    row_count = latents.shape[0]
    outer = lax.axis_size("fy")
    inner = lax.axis_size("fp")
    heads = outer * inner
    per_frame = FRAME_TOK // row_count
    shard = lax.axis_index("fy") * inner + lax.axis_index("fp")

    chunks = head_chunks(jnp.transpose(projected, (1, 0, 2)), heads)
    qkv = lax.all_to_all(chunks, ("fy", "fp"), split_axis=0, concat_axis=0, tiled=True)
    def shifted(value, shift):
        pairs = [(source, (source + shift) % outer) for source in range(outer)]
        return lax.ppermute(value, "fy", pairs)

    half = out_weight.shape[0] // 2
    from_below = shifted(out_weight, 1)
    from_above = shifted(out_weight, -1)
    far_low = shifted(from_below[:half], 1)
    far_high = shifted(from_above[half:], -1)
    shards = [out_weight, from_below, (far_low, far_high), from_above]
    me_outer = lax.axis_index("fy")
    place = ((me_outer - jnp.arange(outer, dtype=jnp.int32)) % outer).astype(jnp.int32)
    halo = passed_along(qkv[per_frame:, 1:3], "tm", 1)
    flag = (lax.axis_index("tm") > 0).astype(jnp.int32).reshape(1)
    spread = attend(flag, qkv, halo, outer, inner)
    spread, near = lax.optimization_barrier((spread, (shards[1], shards[3])))
    shards = [shards[0], near[0], shards[2], near[1]]

    gathered = lax.all_to_all(spread, ("fy", "fp"), split_axis=0, concat_axis=0, tiled=True)
    flat = [shards[0], shards[1], shards[2][0], shards[2][1], shards[3]]
    total = project(place, gathered, [jnp.transpose(shard_w) for shard_w in flat], inner)
    returned = lax.all_to_all(total, "fp", split_axis=0, concat_axis=0, tiled=True)

    frame_index = (shard * row_count) // FRAME_TOK
    gate_row = lax.dynamic_index_in_dim(gate_table, timesteps[frame_index], 0, keepdims=True)
    return finish(returned, latents, gate_row)


def solution(mesh):
    tm_size, fsdp_size = mesh.devices.shape
    split_mesh = Mesh(mesh.devices.reshape(tm_size, fsdp_size // 4, 4), ("tm", "fy", "fp"))
    rows = ("tm", "fy", "fp")
    in_specs = (
        P(rows, None),
        P(rows, None, None),
        P(None, ("fy", "fp")),
        P(),
        P("tm"),
    )
    out_specs = P(rows, None)
    return jax.shard_map(
        body, mesh=split_mesh, in_specs=in_specs, out_specs=out_specs, check_vma=False
    )
```

```python
import functools

import jax
import jax.numpy as jnp
from jax import lax
from jax.experimental import pallas as pl
from jax.experimental.pallas import tpu as pltpu
from jax.sharding import Mesh
from jax.sharding import PartitionSpec as P

FRAME_TOK = 256
WINDOW = 4


def passed_along(value, axis, steps):
    count = lax.axis_size(axis)
    initial, last = (max(0, -steps), min(count, count - steps))
    return lax.ppermute(value, axis, [(source, source + steps) for source in range(initial, last)])


def attention_kernel(frames, flag_ref, qkv_ref, halo_ref, *refs):
    out_ref = refs[-1]
    if len(refs) > 1:
        out_ref[...] = refs[0][...]
    row_count = qkv_ref.shape[2]
    per_frame = FRAME_TOK // row_count
    frame_count = qkv_ref.shape[0] // per_frame
    score_scale = qkv_ref.shape[3] ** (-0.5)
    inner = out_ref.shape[0] // frame_count
    has_prev = flag_ref[0] > 0

    def frame_rows(ref, block, plane):
        return ref[pl.ds(block, per_frame), plane].reshape(FRAME_TOK, ref.shape[3])

    for frame in frames:
        query = frame_rows(qkv_ref, frame * per_frame, 0)
        blocks = []
        for back in range(WINDOW):
            source = frame - (WINDOW - 1) + back
            if source >= 0:
                key = frame_rows(qkv_ref, source * per_frame, 1)
                value = frame_rows(qkv_ref, source * per_frame, 2)
            else:
                block = (source + WINDOW - 1) * per_frame
                key, value = frame_rows(halo_ref, block, 0), frame_rows(halo_ref, block, 1)
            scores = (
                lax.dot_general(
                    query, key, (((1,), (1,)), ((), ())), preferred_element_type=jnp.float32
                )
                * score_scale
            )
            if source < 0:
                scores = jnp.where(has_prev, scores, -1e30)
            blocks.append((scores, value))
        row_max = blocks[0][0].max(axis=1, keepdims=True)
        for scores, _ in blocks[1:]:
            row_max = jnp.maximum(row_max, scores.max(axis=1, keepdims=True))
        weights = [jnp.exp(scores - row_max) for scores, _ in blocks]
        row_sum = weights[0].sum(axis=1, keepdims=True)
        for w in weights[1:]:
            row_sum = row_sum + w.sum(axis=1, keepdims=True)
        inverse = 1.0 / row_sum
        total = None
        for w, (_, value) in zip(weights, blocks):
            probability = (w * inverse).astype(jnp.bfloat16)
            part = jnp.dot(probability, value, preferred_element_type=jnp.float32)
            total = part if total is None else total + part
        total = total.astype(out_ref.dtype)
        for dest in range(frame * inner, (frame + 1) * inner):
            out_ref[dest] = total


def attend(flag, qkv, halo, outer, inner):
    width = qkv.shape[3]
    frame_count = qkv.shape[0] * qkv.shape[2] // FRAME_TOK
    vmem = pl.BlockSpec(memory_space=pltpu.VMEM)
    smem = pl.BlockSpec(memory_space=pltpu.SMEM)
    out_shape = jax.ShapeDtypeStruct((outer * inner, FRAME_TOK, width), jnp.bfloat16)
    local = tuple(range(WINDOW - 1, frame_count))
    first = pl.pallas_call(
        functools.partial(attention_kernel, local),
        out_shape=out_shape,
        in_specs=[smem, vmem, vmem],
        out_specs=vmem,
    )(flag, qkv, qkv)
    return pl.pallas_call(
        functools.partial(attention_kernel, tuple(range(WINDOW - 1))),
        out_shape=out_shape,
        in_specs=[smem, vmem, vmem, vmem],
        out_specs=vmem,
        input_output_aliases={3: 0},
    )(flag, qkv, halo, first)


def chunk_kernel(rows_ref, out_ref):
    width = out_ref.shape[3]
    for head in range(out_ref.shape[0]):
        out_ref[head] = rows_ref[:, :, head * width : (head + 1) * width]


def head_chunks(planes, heads):
    lanes, row_count, features = planes.shape
    vmem = pl.BlockSpec(memory_space=pltpu.VMEM)
    return pl.pallas_call(
        chunk_kernel,
        out_shape=jax.ShapeDtypeStruct((heads, lanes, row_count, features // heads), planes.dtype),
        in_specs=[vmem],
        out_specs=vmem,
    )(planes)


def projection_kernel(place_ref, gathered_ref, *refs):
    weight_refs, out_ref = refs[:-1], refs[-1]
    heads, head_dim = gathered_ref.shape[0], gathered_ref.shape[2]
    rows = out_ref.shape[2]
    slots = out_ref.shape[1]
    pieces = [[ref] for ref in weight_refs[:2]] + [list(weight_refs[2:4])] + [[weight_refs[4]]]
    for shift in range(slots):
        parts = pieces[shift]
        per_part = heads // len(parts)
        total = None
        for head in range(heads):
            weight_ref = parts[head // per_part]
            column = (head % per_part) * head_dim
            part = lax.dot_general(
                gathered_ref[head],
                weight_ref[:, column : column + head_dim],
                (((1,), (1,)), ((), ())),
                preferred_element_type=jnp.float32,
            )
            total = part if total is None else total + part
        total = total.astype(out_ref.dtype)
        for group in range(out_ref.shape[0]):
            out_ref[group, place_ref[shift]] = total[group * rows : (group + 1) * rows]


def project(place, gathered, weights_t, groups):
    vmem = pl.BlockSpec(memory_space=pltpu.VMEM)
    count, width = 4, weights_t[0].shape[0]
    rows = gathered.shape[1] // groups
    return pl.pallas_call(
        projection_kernel,
        out_shape=jax.ShapeDtypeStruct((groups, count, rows, width), jnp.bfloat16),
        in_specs=[pl.BlockSpec(memory_space=pltpu.SMEM)] + [vmem] * (len(weights_t) + 1),
        out_specs=vmem,
    )(place, gathered, *weights_t)


def finish_kernel(returned_ref, latents_ref, gate_ref, out_ref):
    senders, blocks, _, width = returned_ref.shape
    for block in range(blocks):
        for sender in range(senders):
            column = width * (senders * block + sender)
            branch = returned_ref[sender, block]
            residual = latents_ref[:, column : column + width].astype(jnp.float32)
            gate = gate_ref[:, column : column + width]
            out_ref[:, column : column + width] = (
                residual + gate * branch.astype(jnp.float32)
            ).astype(out_ref.dtype)


def finish(returned, latents, gate_row):
    vmem = pl.BlockSpec(memory_space=pltpu.VMEM)
    return pl.pallas_call(
        finish_kernel,
        out_shape=jax.ShapeDtypeStruct(latents.shape, jnp.bfloat16),
        in_specs=[vmem, vmem, vmem],
        out_specs=vmem,
    )(returned, latents, gate_row)


def body(latents, projected, out_weight, gate_table, timesteps):
    row_count = latents.shape[0]
    outer = lax.axis_size("fy")
    inner = lax.axis_size("fp")
    heads = outer * inner
    per_frame = FRAME_TOK // row_count
    shard = lax.axis_index("fy") * inner + lax.axis_index("fp")

    chunks = head_chunks(jnp.transpose(projected, (1, 0, 2)), heads)
    qkv = lax.all_to_all(chunks, ("fy", "fp"), split_axis=0, concat_axis=0, tiled=True)
    def shifted(value, shift):
        pairs = [(source, (source + shift) % outer) for source in range(outer)]
        return lax.ppermute(value, "fy", pairs)

    half = out_weight.shape[0] // 2
    from_below = shifted(out_weight, 1)
    from_above = shifted(out_weight, -1)
    far_low = shifted(from_below[:half], 1)
    far_high = shifted(from_above[half:], -1)
    shards = [out_weight, from_below, (far_low, far_high), from_above]
    me_outer = lax.axis_index("fy")
    place = ((me_outer - jnp.arange(outer, dtype=jnp.int32)) % outer).astype(jnp.int32)
    halo = passed_along(qkv[per_frame:, 1:3], "tm", 1)
    flag = (lax.axis_index("tm") > 0).astype(jnp.int32).reshape(1)
    spread = attend(flag, qkv, halo, outer, inner)
    spread, near = lax.optimization_barrier((spread, (shards[1], shards[3])))
    shards = [shards[0], near[0], shards[2], near[1]]

    gathered = lax.all_to_all(spread, ("fy", "fp"), split_axis=0, concat_axis=0, tiled=True)
    flat = [shards[0], shards[1], shards[2][0], shards[2][1], shards[3]]
    total = project(place, gathered, [jnp.transpose(shard_w) for shard_w in flat], inner)
    returned = lax.all_to_all(total, "fp", split_axis=0, concat_axis=0, tiled=True)

    frame_index = (shard * row_count) // FRAME_TOK
    gate_row = lax.dynamic_index_in_dim(gate_table, timesteps[frame_index], 0, keepdims=True)
    return finish(returned, latents, gate_row)


def solution(mesh):
    tm_size, fsdp_size = mesh.devices.shape
    split_mesh = Mesh(mesh.devices.reshape(tm_size, fsdp_size // 4, 4), ("tm", "fy", "fp"))
    rows = ("tm", "fy", "fp")
    in_specs = (
        P(rows, None),
        P(rows, None, None),
        P(None, ("fy", "fp")),
        P(),
        P("tm"),
    )
    out_specs = P(rows, None)
    return jax.shard_map(
        body, mesh=split_mesh, in_specs=in_specs, out_specs=out_specs, check_vma=False
    )
```
